256 devices in a mesh: seq: 16 (over z, y_lo), chan: 16 (over y_hi, x, core).
Axes of the slice: x: 4, y: 4 (y_hi: 2, y_lo: 2; y = y_hi * 2 + y_lo), z: 8, core: 2. Of those that a mesh axis runs over, the one named last changes fastest.
Arguments:
- tokens: bfloat16 [4096, 4096], P('seq', 'chan'), may hold values from -6 to 6
- in_weight: bfloat16 [4096, 3, 4096], P(None, None, 'chan'), may hold values from -0.09375 to 0.09375
- short_weight: float32 [3, 3, 4096], P(None, None, 'chan'), may hold values from -3 to 3
- filter_taps: bfloat16 [4096, 4096], P(None, 'chan'), may hold values from -0.09375 to 0.09375
- cotangent: bfloat16 [4096, 4096], P('seq', 'chan'), may hold values from -1.5 to 1.5
Outputs:
- operator_out: bfloat16 [4096, 4096], P('seq', 'chan')
- stream_grads: bfloat16 [4096, 3, 4096], P('seq', None, 'chan')
- tap_grads: float32 [4096, 4096], P('seq', 'chan')
The draws below stay inside these ranges and needn't reach their ends.
All inputs are finite; a program needn't handle non-finite values.
Results may differ from the reference program's by a relative error of at most 0.015.
Values may be sent and summed in bfloat16 or wider, within the bound.
No kernel may reach another device: no remote copies, remote signals or barrier semaphores. Data moves between devices by JAX's collectives and lax.ppermute only.
A program may use at most 128 MiB of HBM per device.

```python
import math
import jax
import jax.numpy as jnp
from jax import lax

D = 4096
TOK_DEV = 256
L = 4096


def shard_levels(rng, shape, shards, smallest, high):
    gain, own = 1.0, jax.random.fold_in(rng, 6)
    for axis_at, blocks in shards:
        steps = jnp.exp(jax.random.uniform(jax.random.fold_in(own, axis_at), (blocks,), jnp.float32, smallest / len(shards), high / len(shards)))
        gain = gain * jnp.repeat(steps, shape[axis_at] // blocks).reshape([-1 if axis == axis_at else 1 for axis in range(len(shape))])
    return gain


def normal_values(key, dims, width, bound, cuts=(), kind=jnp.bfloat16):
    array = width * jax.random.normal(key, dims, jnp.float32)
    if cuts:
        array = array * shard_levels(key, dims, cuts, -0.22, 0.18)
    return jnp.clip(array, -bound, bound).astype(kind)


def setup_inputs(seed: int = 0) -> dict:
    seeds = jax.random.split(jax.random.key(seed), 6)
    return {
        "tokens": normal_values(seeds[0], (L, D), 1.0, 6.0, ((0, 16), (1, 16))),
        "in_weight": normal_values(seeds[1], (D, 3, D), D ** -0.5, 0.09375, ((2, 16),)),
        "short_weight": normal_values(seeds[2], (3, 3, D), 0.6, 3.0, ((2, 16),), jnp.float32),
        "filter_taps": normal_values(seeds[3], (L, D), L ** -0.5, 0.09375, ((1, 16),)),
        "cotangent": normal_values(seeds[4], (L, D), 0.25, 1.5, ((0, 16), (1, 16))),
    }


def dft_tables(row_count):
    length = 2 * row_count
    sample = jnp.arange(length, dtype=jnp.int32)
    frequency = jnp.arange(row_count, dtype=jnp.int32)
    angles = ((frequency[:, None] * sample[None, :]) % length).astype(jnp.float32) * (2.0 * math.pi / length)
    parity = 1.0 - 2.0 * (sample % 2).astype(jnp.float32)
    lower_rows = jnp.where(frequency[:, None] == 0, parity[None, :], -jnp.sin(angles))
    forward = jnp.concatenate([jnp.cos(angles), lower_rows], axis=0)
    out_index = row_count + frequency
    back_angles = ((out_index[:, None] * frequency[None, :]) % length).astype(jnp.float32) * (2.0 * math.pi / length)
    factor = jnp.where(frequency == 0, 1.0, 2.0) / length
    out_parity = 1.0 - 2.0 * (out_index % 2).astype(jnp.float32)
    real_part = jnp.cos(back_angles) * factor[None, :]
    imag_part = jnp.where(frequency[None, :] == 0, out_parity[:, None] / length, -2.0 * jnp.sin(back_angles) / length)
    inverse = jnp.concatenate([real_part, imag_part], axis=1)
    return forward, inverse


def spectral_product(left_spec, right_spec):
    half_len = left_spec.shape[0] // 2
    left_spec = left_spec.astype(jnp.float32)
    right_spec = right_spec.astype(jnp.float32)
    left_re, left_im = left_spec[:half_len], left_spec[half_len:]
    right_re, right_im = right_spec[:half_len], right_spec[half_len:]
    first_row = (jnp.arange(half_len) == 0).reshape((half_len,) + (1,) * (left_spec.ndim - 1))
    cross_term = left_im * right_im
    real_out = left_re * right_re - jnp.where(first_row, 0.0, cross_term)
    imag_out = jnp.where(first_row, cross_term, left_re * right_im + left_im * right_re)
    return jnp.concatenate([real_out, imag_out], axis=0)


def spectral_adjoint(left_spec, grad_spec):
    half_len = left_spec.shape[0] // 2
    left_spec = left_spec.astype(jnp.float32)
    grad_spec = grad_spec.astype(jnp.float32)
    left_re, left_im = left_spec[:half_len], left_spec[half_len:]
    grad_re, grad_im = grad_spec[:half_len], grad_spec[half_len:]
    first_row = (jnp.arange(half_len) == 0).reshape((half_len,) + (1,) * (left_spec.ndim - 1))
    cross_term = left_im * grad_im
    real_out = left_re * grad_re + jnp.where(first_row, 0.0, cross_term)
    imag_out = jnp.where(first_row, cross_term, left_re * grad_im - left_im * grad_re)
    return jnp.concatenate([real_out, imag_out], axis=0)


def to_cols(values, block_count):
    row_count = values.shape[0] // block_count
    return values.reshape(block_count, row_count, values.shape[1]).transpose(1, 0, 2).reshape(row_count, block_count * values.shape[1])


def from_cols(values, block_count):
    row_count = values.shape[0]
    local_width = values.shape[1] // block_count
    return values.reshape(row_count, block_count, local_width).transpose(1, 0, 2).reshape(block_count * row_count, local_width)


def reference(tokens, in_weight, short_weight, filter_taps, cotangent):
    total_len, model_width = tokens.shape
    row_count = TOK_DEV
    spec_rows = 2 * row_count
    block_count = total_len // row_count
    forward, inverse = dft_tables(row_count)
    full_table = forward.astype(jnp.bfloat16)
    half_table = full_table[:, :row_count]
    back_table = inverse.astype(jnp.bfloat16)

    streams = jnp.dot(tokens, in_weight.reshape(model_width, 3 * model_width), preferred_element_type=jnp.float32).astype(jnp.bfloat16)
    leading = jnp.zeros((2, 3 * model_width), jnp.bfloat16)
    extended = jnp.concatenate([leading, streams], axis=0).astype(jnp.float32).reshape(total_len + 2, 3, model_width)
    conv_out = short_weight[:, 0] * extended[2:] + short_weight[:, 1] * extended[1:-1] + short_weight[:, 2] * extended[:-2]
    query_conv, key_conv, value_conv = conv_out[:, 0], conv_out[:, 1], conv_out[:, 2]
    gated = (key_conv * value_conv).astype(jnp.bfloat16)

    own_spec = jnp.dot(half_table, to_cols(gated, block_count), preferred_element_type=jnp.float32).astype(jnp.bfloat16)
    own_spec = own_spec.reshape(spec_rows, block_count, model_width)
    tap_blocks = filter_taps.reshape(block_count, row_count, model_width)
    earlier = jnp.concatenate([jnp.zeros((1, row_count, model_width), jnp.bfloat16), tap_blocks[:-1]], axis=0)
    segments = jnp.concatenate([earlier, tap_blocks], axis=1).transpose(1, 0, 2).reshape(spec_rows, block_count * model_width)
    filters = jnp.dot(full_table, segments, preferred_element_type=jnp.float32).astype(jnp.bfloat16)
    filters = filters.reshape(spec_rows, block_count, model_width)

    mixed_spec = jnp.zeros((spec_rows, block_count, model_width), jnp.float32)
    for lag_step in range(block_count):
        shifted = jnp.concatenate([jnp.zeros((spec_rows, lag_step, model_width), jnp.bfloat16), own_spec[:, :block_count - lag_step]], axis=1)
        mixed_spec = mixed_spec + spectral_product(filters[:, lag_step:lag_step + 1], shifted)
    long_cols = jnp.dot(back_table, mixed_spec.astype(jnp.bfloat16).reshape(spec_rows, block_count * model_width), preferred_element_type=jnp.float32)
    long_out = from_cols(long_cols.astype(jnp.bfloat16), block_count)

    operator_out = (query_conv * long_out.astype(jnp.float32)).astype(jnp.bfloat16)
    cot_wide = cotangent.astype(jnp.float32)
    grad_long = (cot_wide * query_conv).astype(jnp.bfloat16)
    grad_query = cot_wide * long_out.astype(jnp.float32)

    grad_spec = jnp.dot(back_table.T, to_cols(grad_long, block_count), preferred_element_type=jnp.float32).astype(jnp.bfloat16)
    grad_spec = grad_spec.reshape(spec_rows, block_count, model_width)
    spectral_grad = jnp.zeros((spec_rows, block_count, model_width), jnp.float32)
    filter_parts = []
    for lag_step in range(block_count):
        ahead = jnp.concatenate([grad_spec[:, lag_step:], jnp.zeros((spec_rows, lag_step, model_width), jnp.bfloat16)], axis=1)
        spectral_grad = spectral_grad + spectral_adjoint(filters[:, lag_step:lag_step + 1], ahead)
        filter_parts.append(jnp.sum(spectral_adjoint(own_spec[:, :block_count - lag_step], grad_spec[:, lag_step:]), axis=1))
    filter_grad = jnp.stack(filter_parts, axis=1)
    gated_cols = jnp.dot(half_table.T, spectral_grad.astype(jnp.bfloat16).reshape(spec_rows, block_count * model_width), preferred_element_type=jnp.float32)
    grad_gated = from_cols(gated_cols.astype(jnp.bfloat16), block_count)

    tap_spec = jnp.dot(forward.T, filter_grad.reshape(spec_rows, block_count * model_width), precision=lax.Precision.HIGHEST)
    tap_spec = tap_spec.reshape(spec_rows, block_count, model_width)
    tap_cols = tap_spec[row_count:] + jnp.concatenate([tap_spec[:row_count, 1:], jnp.zeros((row_count, 1, model_width), jnp.float32)], axis=1)
    tap_grads = from_cols(tap_cols.reshape(row_count, block_count * model_width), block_count)

    gated_wide = grad_gated.astype(jnp.float32)
    grad_streams = jnp.stack([grad_query, gated_wide * value_conv, gated_wide * key_conv], axis=1).astype(jnp.bfloat16)
    trailing = jnp.zeros((2, 3, model_width), jnp.bfloat16)
    padded = jnp.concatenate([grad_streams, trailing], axis=0).astype(jnp.float32)
    stream_grads = (short_weight[:, 0] * padded[:total_len] + short_weight[:, 1] * padded[1:total_len + 1] + short_weight[:, 2] * padded[2:]).astype(jnp.bfloat16)
    return (operator_out, stream_grads, tap_grads)
```

```python
import math

import jax
import jax.numpy as jnp
from jax import lax
from jax.sharding import PartitionSpec as P


def passed_along(block, axis, distance):
    devices = range(lax.axis_size(axis))
    route = [(i - distance, i) for i in devices if i - distance in devices]
    return lax.ppermute(block, axis, route)


def dft_tables(row_count):
    length = 2 * row_count
    sample = jnp.arange(length, dtype=jnp.int32)
    frequency = jnp.arange(row_count, dtype=jnp.int32)
    angles = (frequency[:, None] * sample[None, :] % length).astype(jnp.float32) * (
        2.0 * math.pi / length
    )
    parity = 1.0 - 2.0 * (sample % 2).astype(jnp.float32)
    lower_rows = jnp.where(frequency[:, None] == 0, parity[None, :], -jnp.sin(angles))
    forward = jnp.concatenate([jnp.cos(angles), lower_rows], axis=0)
    out_index = row_count + frequency
    back_angles = (out_index[:, None] * frequency[None, :] % length).astype(jnp.float32) * (
        2.0 * math.pi / length
    )
    factor = jnp.where(frequency == 0, 1.0, 2.0) / length
    out_parity = 1.0 - 2.0 * (out_index % 2).astype(jnp.float32)
    real_part = jnp.cos(back_angles) * factor[None, :]
    imag_part = jnp.where(
        frequency[None, :] == 0, out_parity[:, None] / length, -2.0 * jnp.sin(back_angles) / length
    )
    inverse = jnp.concatenate([real_part, imag_part], axis=1)
    return (forward, inverse)


def spectral_product(left_spec, right_spec):
    half_len = left_spec.shape[-1] // 2
    left_spec = left_spec.astype(jnp.float32)
    right_spec = right_spec.astype(jnp.float32)
    left_re, left_im = (left_spec[..., :half_len], left_spec[..., half_len:])
    right_re, right_im = (right_spec[..., :half_len], right_spec[..., half_len:])
    first_row = lax.broadcasted_iota(jnp.int32, (1,) * (left_spec.ndim - 1) + (half_len,), left_spec.ndim - 1) == 0
    cross_term = left_im * right_im
    real_out = left_re * right_re - jnp.where(first_row, 0.0, cross_term)
    imag_out = jnp.where(first_row, cross_term, left_re * right_im + left_im * right_re)
    return jnp.concatenate([real_out, imag_out], axis=-1)


def spectral_adjoint(left_spec, grad_spec):
    half_len = left_spec.shape[-1] // 2
    left_spec = left_spec.astype(jnp.float32)
    grad_spec = grad_spec.astype(jnp.float32)
    left_re, left_im = (left_spec[..., :half_len], left_spec[..., half_len:])
    grad_re, grad_im = (grad_spec[..., :half_len], grad_spec[..., half_len:])
    first_row = lax.broadcasted_iota(jnp.int32, (1,) * (left_spec.ndim - 1) + (half_len,), left_spec.ndim - 1) == 0
    cross_term = left_im * grad_im
    real_out = left_re * grad_re + jnp.where(first_row, 0.0, cross_term)
    imag_out = jnp.where(first_row, cross_term, left_re * grad_im - left_im * grad_re)
    return jnp.concatenate([real_out, imag_out], axis=-1)


def neighbour_rows(edge_rows, offset):
    return passed_along(edge_rows, "seq", offset)


def swap_layout(values):
    return lax.all_to_all(values, "seq", 1, 1, tiled=True)


def on_device(tokens, in_weight, short_weight, filter_taps, cotangent):
    row_count, local_width = tokens.shape
    seq_count = lax.axis_size("seq")
    group = local_width // seq_count
    own_block = lax.axis_index("seq")
    forward, inverse = dft_tables(row_count)
    full_table = forward.astype(jnp.bfloat16)
    half_table = full_table[:, :row_count]
    back_table = inverse.astype(jnp.bfloat16)
    weight_cols = in_weight.reshape(in_weight.shape[0], 3 * local_width)
    streams = jnp.dot(
        lax.all_gather(tokens, "chan", axis=1, tiled=True),
        weight_cols,
        preferred_element_type=jnp.float32,
    )
    streams = streams.astype(jnp.bfloat16)
    before = neighbour_rows(streams[row_count - 2 :], 1)
    extended = (
        jnp.concatenate([before, streams], axis=0)
        .astype(jnp.float32)
        .reshape(row_count + 2, 3, local_width)
    )
    conv_out = (
        short_weight[:, 0] * extended[2:]
        + short_weight[:, 1] * extended[1:-1]
        + short_weight[:, 2] * extended[:-2]
    )
    query_conv, key_conv, value_conv = (conv_out[:, 0], conv_out[:, 1], conv_out[:, 2])
    gated = (key_conv * value_conv).astype(jnp.bfloat16)

    gated_cols = swap_layout(gated.reshape(row_count, seq_count, group))
    own_spec = jnp.einsum(
        "tbc,kt->bck", gated_cols, half_table, preferred_element_type=jnp.float32
    ).astype(jnp.bfloat16)
    own_taps = lax.dynamic_slice_in_dim(filter_taps, own_block * group, group, axis=1)
    tap_blocks = own_taps.reshape(seq_count, row_count, group)
    earlier = jnp.concatenate(
        [jnp.zeros((1, row_count, group), jnp.bfloat16), tap_blocks[:-1]], axis=0
    )
    segments = jnp.concatenate([earlier, tap_blocks], axis=1)
    filters = jnp.einsum(
        "fn,bnc->bcf", full_table, segments, preferred_element_type=jnp.float32
    ).astype(jnp.bfloat16)

    mixed_spec = jnp.zeros(own_spec.shape, jnp.float32)
    for lag_step in range(seq_count):
        term = spectral_product(filters[lag_step][None], own_spec[: seq_count - lag_step])
        mixed_spec = mixed_spec + jnp.pad(term, ((lag_step, 0), (0, 0), (0, 0)))
    long_cols = jnp.einsum(
        "bck,ak->abc", mixed_spec.astype(jnp.bfloat16), back_table,
        preferred_element_type=jnp.float32,
    ).astype(jnp.bfloat16)
    long_out = swap_layout(long_cols).reshape(row_count, local_width)

    operator_out = (query_conv * long_out.astype(jnp.float32)).astype(jnp.bfloat16)
    cot_wide = cotangent.astype(jnp.float32)
    grad_long = (cot_wide * query_conv).astype(jnp.bfloat16)
    grad_query = cot_wide * long_out.astype(jnp.float32)

    grad_long_cols = swap_layout(grad_long.reshape(row_count, seq_count, group))
    grad_spec = jnp.einsum(
        "abc,ak->bck", grad_long_cols, back_table, preferred_element_type=jnp.float32
    ).astype(jnp.bfloat16)
    spectral_grad = jnp.zeros(grad_spec.shape, jnp.float32)
    filter_parts = []
    for lag_step in range(seq_count):
        ahead = grad_spec[lag_step:]
        term = spectral_adjoint(filters[lag_step][None], ahead)
        spectral_grad = spectral_grad + jnp.pad(term, ((0, lag_step), (0, 0), (0, 0)))
        filter_parts.append(
            jnp.sum(spectral_adjoint(own_spec[: seq_count - lag_step], ahead), axis=0)
        )
    filter_grad = jnp.stack(filter_parts, axis=0)
    gated_grad_cols = jnp.einsum(
        "bck,kt->tbc", spectral_grad.astype(jnp.bfloat16), half_table,
        preferred_element_type=jnp.float32,
    ).astype(jnp.bfloat16)
    grad_gated = swap_layout(gated_grad_cols).reshape(row_count, local_width)

    tap_spec = jnp.einsum("dck,kn->dcn", filter_grad, forward, precision=lax.Precision.HIGHEST)
    tap_cols = tap_spec[:, :, row_count:] + jnp.concatenate(
        [tap_spec[1:, :, :row_count], jnp.zeros((1, group, row_count), jnp.float32)], axis=0
    )
    tap_grads = swap_layout(tap_cols.transpose(2, 0, 1)).reshape(row_count, local_width)

    gated_wide = grad_gated.astype(jnp.float32)
    grad_streams = jnp.stack(
        [grad_query, gated_wide * value_conv, gated_wide * key_conv], axis=1
    ).astype(jnp.bfloat16)
    grad_streams = grad_streams.reshape(row_count, 3 * local_width)
    after = neighbour_rows(grad_streams[:2], -1)
    padded = (
        jnp.concatenate([grad_streams, after], axis=0)
        .astype(jnp.float32)
        .reshape(row_count + 2, 3, local_width)
    )
    stream_grads = (
        short_weight[:, 0] * padded[:row_count]
        + short_weight[:, 1] * padded[1 : row_count + 1]
        + short_weight[:, 2] * padded[2:]
    ).astype(jnp.bfloat16)
    return (operator_out, stream_grads, tap_grads)


def solution(mesh):
    return jax.shard_map(
        on_device,
        mesh=mesh,
        in_specs=(
            P("seq", "chan"),
            P(None, None, "chan"),
            P(None, None, "chan"),
            P(None, "chan"),
            P("seq", "chan"),
        ),
        out_specs=(P("seq", "chan"), P("seq", None, "chan"), P("seq", "chan")),
        check_vma=False,
    )
```

```python
import math

import jax
import jax.numpy as jnp
from jax import lax
from jax.sharding import PartitionSpec as P


def passed_along(block, axis, distance):
    devices = range(lax.axis_size(axis))
    route = [(i - distance, i) for i in devices if i - distance in devices]
    return lax.ppermute(block, axis, route)


def dft_tables(row_count):
    length = 2 * row_count
    sample = jnp.arange(length, dtype=jnp.int32)
    frequency = jnp.arange(row_count, dtype=jnp.int32)
    angles = (frequency[:, None] * sample[None, :] % length).astype(jnp.float32) * (
        2.0 * math.pi / length
    )
    parity = 1.0 - 2.0 * (sample % 2).astype(jnp.float32)
    lower_rows = jnp.where(frequency[:, None] == 0, parity[None, :], -jnp.sin(angles))
    forward = jnp.concatenate([jnp.cos(angles), lower_rows], axis=0)
    out_index = row_count + frequency
    back_angles = (out_index[:, None] * frequency[None, :] % length).astype(jnp.float32) * (
        2.0 * math.pi / length
    )
    factor = jnp.where(frequency == 0, 1.0, 2.0) / length
    out_parity = 1.0 - 2.0 * (out_index % 2).astype(jnp.float32)
    real_part = jnp.cos(back_angles) * factor[None, :]
    imag_part = jnp.where(
        frequency[None, :] == 0, out_parity[:, None] / length, -2.0 * jnp.sin(back_angles) / length
    )
    inverse = jnp.concatenate([real_part, imag_part], axis=1)
    return (forward, inverse)


def spectral_product(left_spec, right_spec):
    half_len = left_spec.shape[-1] // 2
    left_spec = left_spec.astype(jnp.float32)
    right_spec = right_spec.astype(jnp.float32)
    left_re, left_im = (left_spec[..., :half_len], left_spec[..., half_len:])
    right_re, right_im = (right_spec[..., :half_len], right_spec[..., half_len:])
    first_row = lax.broadcasted_iota(jnp.int32, (1,) * (left_spec.ndim - 1) + (half_len,), left_spec.ndim - 1) == 0
    cross_term = left_im * right_im
    real_out = left_re * right_re - jnp.where(first_row, 0.0, cross_term)
    imag_out = jnp.where(first_row, cross_term, left_re * right_im + left_im * right_re)
    return jnp.concatenate([real_out, imag_out], axis=-1)


def spectral_adjoint(left_spec, grad_spec):
    half_len = left_spec.shape[-1] // 2
    left_spec = left_spec.astype(jnp.float32)
    grad_spec = grad_spec.astype(jnp.float32)
    left_re, left_im = (left_spec[..., :half_len], left_spec[..., half_len:])
    grad_re, grad_im = (grad_spec[..., :half_len], grad_spec[..., half_len:])
    first_row = lax.broadcasted_iota(jnp.int32, (1,) * (left_spec.ndim - 1) + (half_len,), left_spec.ndim - 1) == 0
    cross_term = left_im * grad_im
    real_out = left_re * grad_re + jnp.where(first_row, 0.0, cross_term)
    imag_out = jnp.where(first_row, cross_term, left_re * grad_im - left_im * grad_re)
    return jnp.concatenate([real_out, imag_out], axis=-1)


def neighbour_rows(edge_rows, offset):
    return passed_along(edge_rows, "seq", offset)


def swap_layout(values):
    return lax.all_to_all(values, "seq", 1, 1, tiled=True)


def on_device(tokens, in_weight, short_weight, filter_taps, cotangent):
    row_count, local_width = tokens.shape
    seq_count = lax.axis_size("seq")
    group = local_width // seq_count
    own_block = lax.axis_index("seq")
    forward, inverse = dft_tables(row_count)
    full_table = forward.astype(jnp.bfloat16)
    half_table = full_table[:, :row_count]
    back_table = inverse.astype(jnp.bfloat16)
    chan_count = lax.axis_size("chan")
    copies = jnp.broadcast_to(tokens[None], (chan_count,) + tokens.shape)
    gathered = lax.all_to_all(copies, "chan", 0, 0, tiled=True)
    weight_parts = in_weight.reshape(chan_count, local_width, 3, local_width)
    streams = jnp.einsum(
        "stf,sfqc->tqc", gathered, weight_parts, preferred_element_type=jnp.float32
    ).astype(jnp.bfloat16)
    streams = streams.reshape(row_count, 3 * local_width)
    before = neighbour_rows(streams[row_count - 2 :], 1)
    extended = (
        jnp.concatenate([before, streams], axis=0)
        .astype(jnp.float32)
        .reshape(row_count + 2, 3, local_width)
    )
    conv_out = (
        short_weight[:, 0] * extended[2:]
        + short_weight[:, 1] * extended[1:-1]
        + short_weight[:, 2] * extended[:-2]
    )
    query_conv, key_conv, value_conv = (conv_out[:, 0], conv_out[:, 1], conv_out[:, 2])
    gated = (key_conv * value_conv).astype(jnp.bfloat16)
    cot_wide = cotangent.astype(jnp.float32)
    grad_long = (cot_wide * query_conv).astype(jnp.bfloat16)

    both_cols = swap_layout(
        jnp.concatenate(
            [gated.reshape(row_count, seq_count, group), grad_long.reshape(row_count, seq_count, group)],
            axis=2,
        )
    )
    gated_cols, grad_long_cols = (both_cols[..., :group], both_cols[..., group:])
    own_spec = jnp.einsum(
        "tbc,kt->bck", gated_cols, half_table, preferred_element_type=jnp.float32
    ).astype(jnp.bfloat16)
    own_taps = lax.dynamic_slice_in_dim(filter_taps, own_block * group, group, axis=1)
    tap_blocks = own_taps.reshape(seq_count, row_count, group)
    earlier = jnp.concatenate(
        [jnp.zeros((1, row_count, group), jnp.bfloat16), tap_blocks[:-1]], axis=0
    )
    segments = jnp.concatenate([earlier, tap_blocks], axis=1)
    filters = jnp.einsum(
        "fn,bnc->bcf", full_table, segments, preferred_element_type=jnp.float32
    ).astype(jnp.bfloat16)

    mixed_spec = jnp.zeros(own_spec.shape, jnp.float32)
    for lag_step in range(seq_count):
        term = spectral_product(filters[lag_step][None], own_spec[: seq_count - lag_step])
        mixed_spec = mixed_spec + jnp.pad(term, ((lag_step, 0), (0, 0), (0, 0)))
    long_cols = jnp.einsum(
        "bck,ak->abc", mixed_spec.astype(jnp.bfloat16), back_table,
        preferred_element_type=jnp.float32,
    ).astype(jnp.bfloat16)

    grad_spec = jnp.einsum(
        "abc,ak->bck", grad_long_cols, back_table, preferred_element_type=jnp.float32
    ).astype(jnp.bfloat16)
    spectral_grad = jnp.zeros(grad_spec.shape, jnp.float32)
    filter_parts = []
    for lag_step in range(seq_count):
        ahead = grad_spec[lag_step:]
        term = spectral_adjoint(filters[lag_step][None], ahead)
        spectral_grad = spectral_grad + jnp.pad(term, ((0, lag_step), (0, 0), (0, 0)))
        filter_parts.append(
            jnp.sum(spectral_adjoint(own_spec[: seq_count - lag_step], ahead), axis=0)
        )
    filter_grad = jnp.stack(filter_parts, axis=0)
    gated_grad_cols = jnp.einsum(
        "bck,kt->tbc", spectral_grad.astype(jnp.bfloat16), half_table,
        preferred_element_type=jnp.float32,
    ).astype(jnp.bfloat16)

    tap_spec = jnp.einsum("dck,kn->dcn", filter_grad, forward, precision=lax.Precision.HIGHEST)
    tap_cols = tap_spec[:, :, row_count:] + jnp.concatenate(
        [tap_spec[1:, :, :row_count], jnp.zeros((1, group, row_count), jnp.float32)], axis=0
    )
    returned = swap_layout(
        jnp.concatenate(
            [
                long_cols.astype(jnp.float32),
                gated_grad_cols.astype(jnp.float32),
                tap_cols.transpose(2, 0, 1),
            ],
            axis=2,
        )
    )
    long_out = returned[..., :group].reshape(row_count, local_width)
    gated_wide = returned[..., group : 2 * group].reshape(row_count, local_width)
    tap_grads = returned[..., 2 * group :].reshape(row_count, local_width)

    operator_out = (query_conv * long_out).astype(jnp.bfloat16)
    grad_query = cot_wide * long_out

    grad_streams = jnp.stack(
        [grad_query, gated_wide * value_conv, gated_wide * key_conv], axis=1
    ).astype(jnp.bfloat16)
    grad_streams = grad_streams.reshape(row_count, 3 * local_width)
    after = neighbour_rows(grad_streams[:2], -1)
    padded = (
        jnp.concatenate([grad_streams, after], axis=0)
        .astype(jnp.float32)
        .reshape(row_count + 2, 3, local_width)
    )
    stream_grads = (
        short_weight[:, 0] * padded[:row_count]
        + short_weight[:, 1] * padded[1 : row_count + 1]
        + short_weight[:, 2] * padded[2:]
    ).astype(jnp.bfloat16)
    return (operator_out, stream_grads, tap_grads)


def solution(mesh):
    return jax.shard_map(
        on_device,
        mesh=mesh,
        in_specs=(
            P("seq", "chan"),
            P(None, None, "chan"),
            P(None, None, "chan"),
            P(None, "chan"),
            P("seq", "chan"),
        ),
        out_specs=(P("seq", "chan"), P("seq", None, "chan"), P("seq", "chan")),
        check_vma=False,
    )
```

```python
import math

import jax
import jax.numpy as jnp
from jax import lax
from jax.sharding import PartitionSpec as P


def passed_along(block, axis, distance):
    devices = range(lax.axis_size(axis))
    route = [(i - distance, i) for i in devices if i - distance in devices]
    return lax.ppermute(block, axis, route)


def dft_tables(row_count):
    length = 2 * row_count
    sample = jnp.arange(length, dtype=jnp.int32)
    frequency = jnp.arange(row_count, dtype=jnp.int32)
    angles = (frequency[:, None] * sample[None, :] % length).astype(jnp.float32) * (
        2.0 * math.pi / length
    )
    parity = 1.0 - 2.0 * (sample % 2).astype(jnp.float32)
    lower_rows = jnp.where(frequency[:, None] == 0, parity[None, :], -jnp.sin(angles))
    forward = jnp.concatenate([jnp.cos(angles), lower_rows], axis=0)
    out_index = row_count + frequency
    back_angles = (out_index[:, None] * frequency[None, :] % length).astype(jnp.float32) * (
        2.0 * math.pi / length
    )
    factor = jnp.where(frequency == 0, 1.0, 2.0) / length
    out_parity = 1.0 - 2.0 * (out_index % 2).astype(jnp.float32)
    real_part = jnp.cos(back_angles) * factor[None, :]
    imag_part = jnp.where(
        frequency[None, :] == 0, out_parity[:, None] / length, -2.0 * jnp.sin(back_angles) / length
    )
    inverse = jnp.concatenate([real_part, imag_part], axis=1)
    return (forward, inverse)


def spectral_product(left_spec, right_spec):
    half_len = left_spec.shape[-1] // 2
    left_spec = left_spec.astype(jnp.float32)
    right_spec = right_spec.astype(jnp.float32)
    left_re, left_im = (left_spec[..., :half_len], left_spec[..., half_len:])
    right_re, right_im = (right_spec[..., :half_len], right_spec[..., half_len:])
    first_row = lax.broadcasted_iota(jnp.int32, (1,) * (left_spec.ndim - 1) + (half_len,), left_spec.ndim - 1) == 0
    cross_term = left_im * right_im
    real_out = left_re * right_re - jnp.where(first_row, 0.0, cross_term)
    imag_out = jnp.where(first_row, cross_term, left_re * right_im + left_im * right_re)
    return jnp.concatenate([real_out, imag_out], axis=-1)


def spectral_adjoint(left_spec, grad_spec):
    half_len = left_spec.shape[-1] // 2
    left_spec = left_spec.astype(jnp.float32)
    grad_spec = grad_spec.astype(jnp.float32)
    left_re, left_im = (left_spec[..., :half_len], left_spec[..., half_len:])
    grad_re, grad_im = (grad_spec[..., :half_len], grad_spec[..., half_len:])
    first_row = lax.broadcasted_iota(jnp.int32, (1,) * (left_spec.ndim - 1) + (half_len,), left_spec.ndim - 1) == 0
    cross_term = left_im * grad_im
    real_out = left_re * grad_re + jnp.where(first_row, 0.0, cross_term)
    imag_out = jnp.where(first_row, cross_term, left_re * grad_im - left_im * grad_re)
    return jnp.concatenate([real_out, imag_out], axis=-1)


def neighbour_rows(edge_rows, offset):
    return passed_along(edge_rows, "seq", offset)


def swap_layout(values):
    return lax.all_to_all(values, "seq", 1, 1, tiled=True)


def on_device(tokens, in_weight, short_weight, filter_taps, cotangent):
    row_count, local_width = tokens.shape
    seq_count = lax.axis_size("seq")
    chan_count = lax.axis_size("chan")
    group = local_width // seq_count
    own_block = lax.axis_index("seq")
    forward, inverse = dft_tables(row_count)
    full_table = forward.astype(jnp.bfloat16)
    half_table = full_table[:, :row_count]
    back_table = inverse.astype(jnp.bfloat16)

    prev_tokens = neighbour_rows(tokens[row_count - 2 :], 1)
    next_rows = neighbour_rows(jnp.concatenate([tokens[:2], cotangent[:2]], axis=1), -1)
    next_tokens, next_cot = (next_rows[:, :local_width], next_rows[:, local_width:])
    edge_tokens = lax.all_gather(
        jnp.concatenate([prev_tokens, next_tokens], axis=0), "chan", axis=0, tiled=False
    )
    copies = jnp.broadcast_to(tokens[None], (chan_count,) + tokens.shape)
    gathered = lax.all_to_all(copies, "chan", 0, 0, tiled=True)
    weight_parts = in_weight.reshape(chan_count, local_width, 3, local_width)
    streams = jnp.einsum(
        "stf,sfqc->tqc", gathered, weight_parts, preferred_element_type=jnp.float32
    ).astype(jnp.bfloat16)
    edge_streams = jnp.einsum(
        "stf,sfqc->tqc", edge_tokens, weight_parts, preferred_element_type=jnp.float32
    ).astype(jnp.bfloat16)
    extended = jnp.concatenate([edge_streams[:2], streams, edge_streams[2:]], axis=0).astype(
        jnp.float32
    )
    conv_out = (
        short_weight[:, 0] * extended[2:]
        + short_weight[:, 1] * extended[1:-1]
        + short_weight[:, 2] * extended[:-2]
    )
    query_conv, key_conv, value_conv = (conv_out[:, 0], conv_out[:, 1], conv_out[:, 2])
    gated = (key_conv[:row_count] * value_conv[:row_count]).astype(jnp.bfloat16)
    cot_wide = jnp.concatenate([cotangent, next_cot], axis=0).astype(jnp.float32)
    grad_long = (cot_wide[:row_count] * query_conv[:row_count]).astype(jnp.bfloat16)

    both_cols = swap_layout(
        jnp.concatenate(
            [gated.reshape(row_count, seq_count, group), grad_long.reshape(row_count, seq_count, group)],
            axis=2,
        )
    )
    gated_cols, grad_long_cols = (both_cols[..., :group], both_cols[..., group:])
    own_spec = jnp.einsum(
        "tbc,kt->bck", gated_cols, half_table, preferred_element_type=jnp.float32
    ).astype(jnp.bfloat16)
    own_taps = lax.dynamic_slice_in_dim(filter_taps, own_block * group, group, axis=1)
    tap_blocks = own_taps.reshape(seq_count, row_count, group)
    earlier = jnp.concatenate(
        [jnp.zeros((1, row_count, group), jnp.bfloat16), tap_blocks[:-1]], axis=0
    )
    segments = jnp.concatenate([earlier, tap_blocks], axis=1)
    filters = jnp.einsum(
        "fn,bnc->bcf", full_table, segments, preferred_element_type=jnp.float32
    ).astype(jnp.bfloat16)

    mixed_spec = jnp.zeros(own_spec.shape, jnp.float32)
    for lag_step in range(seq_count):
        term = spectral_product(filters[lag_step][None], own_spec[: seq_count - lag_step])
        mixed_spec = mixed_spec + jnp.pad(term, ((lag_step, 0), (0, 0), (0, 0)))
    long_cols = jnp.einsum(
        "bck,ak->abc", mixed_spec.astype(jnp.bfloat16), back_table,
        preferred_element_type=jnp.float32,
    ).astype(jnp.bfloat16)

    grad_spec = jnp.einsum(
        "abc,ak->bck", grad_long_cols, back_table, preferred_element_type=jnp.float32
    ).astype(jnp.bfloat16)
    spectral_grad = jnp.zeros(grad_spec.shape, jnp.float32)
    filter_parts = []
    for lag_step in range(seq_count):
        ahead = grad_spec[lag_step:]
        term = spectral_adjoint(filters[lag_step][None], ahead)
        spectral_grad = spectral_grad + jnp.pad(term, ((0, lag_step), (0, 0), (0, 0)))
        filter_parts.append(
            jnp.sum(spectral_adjoint(own_spec[: seq_count - lag_step], ahead), axis=0)
        )
    filter_grad = jnp.stack(filter_parts, axis=0)
    gated_grad_cols = jnp.einsum(
        "bck,kt->tbc", spectral_grad.astype(jnp.bfloat16), half_table,
        preferred_element_type=jnp.float32,
    ).astype(jnp.bfloat16)

    tap_spec = jnp.einsum("dck,kn->dcn", filter_grad, forward, precision=lax.Precision.HIGHEST)
    tap_cols = tap_spec[:, :, row_count:] + jnp.concatenate(
        [tap_spec[1:, :, :row_count], jnp.zeros((1, group, row_count), jnp.float32)], axis=0
    )
    tap_cols = tap_cols.transpose(2, 0, 1)
    tap_high = tap_cols.astype(jnp.bfloat16)
    tap_low = (tap_cols - tap_high.astype(jnp.float32)).astype(jnp.bfloat16)

    def with_next_rows(cols):
        following = jnp.concatenate(
            [cols[:2, 1:], jnp.zeros((2, 1, group), cols.dtype)], axis=1
        )
        return jnp.concatenate([cols, following], axis=0)

    edge_pad = jnp.zeros((2, seq_count, group), jnp.bfloat16)
    returned = swap_layout(
        jnp.concatenate(
            [
                with_next_rows(long_cols),
                with_next_rows(gated_grad_cols),
                jnp.concatenate([tap_high, edge_pad], axis=0),
                jnp.concatenate([tap_low, edge_pad], axis=0),
            ],
            axis=2,
        )
    )
    wide_rows = row_count + 2
    long_out = returned[..., :group].reshape(wide_rows, local_width).astype(jnp.float32)
    gated_wide = returned[..., group : 2 * group].reshape(wide_rows, local_width).astype(jnp.float32)
    tap_grads = (
        returned[:row_count, :, 2 * group : 3 * group].astype(jnp.float32)
        + returned[:row_count, :, 3 * group :].astype(jnp.float32)
    ).reshape(row_count, local_width)

    operator_out = (query_conv[:row_count] * long_out[:row_count]).astype(jnp.bfloat16)
    grad_query = cot_wide * long_out
    grad_streams = jnp.stack(
        [grad_query, gated_wide * value_conv, gated_wide * key_conv], axis=1
    ).astype(jnp.bfloat16).astype(jnp.float32)
    stream_grads = (
        short_weight[:, 0] * grad_streams[:row_count]
        + short_weight[:, 1] * grad_streams[1 : row_count + 1]
        + short_weight[:, 2] * grad_streams[2:]
    ).astype(jnp.bfloat16)
    return (operator_out, stream_grads, tap_grads)


def solution(mesh):
    return jax.shard_map(
        on_device,
        mesh=mesh,
        in_specs=(
            P("seq", "chan"),
            P(None, None, "chan"),
            P(None, None, "chan"),
            P(None, "chan"),
            P("seq", "chan"),
        ),
        out_specs=(P("seq", "chan"), P("seq", None, "chan"), P("seq", "chan")),
        check_vma=False,
    )
```

```python
import math

import jax
import jax.numpy as jnp
from jax import lax
from jax.sharding import PartitionSpec as P


def passed_along(block, axis, distance):
    devices = range(lax.axis_size(axis))
    route = [(i - distance, i) for i in devices if i - distance in devices]
    return lax.ppermute(block, axis, route)


def dft_tables(row_count):
    length = 2 * row_count
    sample = jnp.arange(length, dtype=jnp.int32)
    frequency = jnp.arange(row_count, dtype=jnp.int32)
    angles = (frequency[:, None] * sample[None, :] % length).astype(jnp.float32) * (
        2.0 * math.pi / length
    )
    parity = 1.0 - 2.0 * (sample % 2).astype(jnp.float32)
    lower_rows = jnp.where(frequency[:, None] == 0, parity[None, :], -jnp.sin(angles))
    forward = jnp.concatenate([jnp.cos(angles), lower_rows], axis=0)
    out_index = row_count + frequency
    back_angles = (out_index[:, None] * frequency[None, :] % length).astype(jnp.float32) * (
        2.0 * math.pi / length
    )
    factor = jnp.where(frequency == 0, 1.0, 2.0) / length
    out_parity = 1.0 - 2.0 * (out_index % 2).astype(jnp.float32)
    real_part = jnp.cos(back_angles) * factor[None, :]
    imag_part = jnp.where(
        frequency[None, :] == 0, out_parity[:, None] / length, -2.0 * jnp.sin(back_angles) / length
    )
    inverse = jnp.concatenate([real_part, imag_part], axis=1)
    return (forward, inverse)


def spectral_product(left_spec, right_spec):
    half_len = left_spec.shape[-1] // 2
    left_spec = left_spec.astype(jnp.float32)
    right_spec = right_spec.astype(jnp.float32)
    left_re, left_im = (left_spec[..., :half_len], left_spec[..., half_len:])
    right_re, right_im = (right_spec[..., :half_len], right_spec[..., half_len:])
    first_row = lax.broadcasted_iota(jnp.int32, (1,) * (left_spec.ndim - 1) + (half_len,), left_spec.ndim - 1) == 0
    cross_term = left_im * right_im
    real_out = left_re * right_re - jnp.where(first_row, 0.0, cross_term)
    imag_out = jnp.where(first_row, cross_term, left_re * right_im + left_im * right_re)
    return jnp.concatenate([real_out, imag_out], axis=-1)


def spectral_adjoint(left_spec, grad_spec):
    half_len = left_spec.shape[-1] // 2
    left_spec = left_spec.astype(jnp.float32)
    grad_spec = grad_spec.astype(jnp.float32)
    left_re, left_im = (left_spec[..., :half_len], left_spec[..., half_len:])
    grad_re, grad_im = (grad_spec[..., :half_len], grad_spec[..., half_len:])
    first_row = lax.broadcasted_iota(jnp.int32, (1,) * (left_spec.ndim - 1) + (half_len,), left_spec.ndim - 1) == 0
    cross_term = left_im * grad_im
    real_out = left_re * grad_re + jnp.where(first_row, 0.0, cross_term)
    imag_out = jnp.where(first_row, cross_term, left_re * grad_im - left_im * grad_re)
    return jnp.concatenate([real_out, imag_out], axis=-1)


def neighbour_rows(edge_rows, offset):
    return passed_along(edge_rows, "seq", offset)


def swap_layout(values):
    return lax.all_to_all(values, "seq", 1, 1, tiled=True)


def on_device(tokens, in_weight, short_weight, filter_taps, cotangent):
    row_count, local_width = tokens.shape
    seq_count = lax.axis_size("seq")
    group = local_width // seq_count
    own_block = lax.axis_index("seq")
    forward, inverse = dft_tables(row_count)
    full_table = forward.astype(jnp.bfloat16)
    half_table = full_table[:, :row_count]
    back_table = inverse.astype(jnp.bfloat16)
    chan_count = lax.axis_size("chan")
    split_rows = row_count // 2
    offloaded = lax.all_gather(tokens[:split_rows], "chan", axis=1, tiled=True)
    copies = jnp.broadcast_to(tokens[None, split_rows:], (chan_count, row_count - split_rows, local_width))
    gathered = lax.all_to_all(copies, "chan", 0, 0, tiled=True)
    weight_parts = in_weight.reshape(chan_count, local_width, 3, local_width)
    streams = jnp.concatenate(
        [
            jnp.einsum(
                "tsf,sfqc->tqc",
                offloaded.reshape(split_rows, chan_count, local_width),
                weight_parts,
                preferred_element_type=jnp.float32,
            ),
            jnp.einsum(
                "stf,sfqc->tqc", gathered, weight_parts, preferred_element_type=jnp.float32
            ),
        ],
        axis=0,
    ).astype(jnp.bfloat16)
    streams = streams.reshape(row_count, 3 * local_width)
    before = neighbour_rows(streams[row_count - 2 :], 1)
    extended = (
        jnp.concatenate([before, streams], axis=0)
        .astype(jnp.float32)
        .reshape(row_count + 2, 3, local_width)
    )
    conv_out = (
        short_weight[:, 0] * extended[2:]
        + short_weight[:, 1] * extended[1:-1]
        + short_weight[:, 2] * extended[:-2]
    )
    query_conv, key_conv, value_conv = (conv_out[:, 0], conv_out[:, 1], conv_out[:, 2])
    gated = (key_conv * value_conv).astype(jnp.bfloat16)
    cot_wide = cotangent.astype(jnp.float32)
    grad_long = (cot_wide * query_conv).astype(jnp.bfloat16)

    both_cols = swap_layout(
        jnp.concatenate(
            [gated.reshape(row_count, seq_count, group), grad_long.reshape(row_count, seq_count, group)],
            axis=2,
        )
    )
    gated_cols, grad_long_cols = (both_cols[..., :group], both_cols[..., group:])
    own_spec = jnp.einsum(
        "tbc,kt->bck", gated_cols, half_table, preferred_element_type=jnp.float32
    ).astype(jnp.bfloat16)
    own_taps = lax.dynamic_slice_in_dim(filter_taps, own_block * group, group, axis=1)
    tap_blocks = own_taps.reshape(seq_count, row_count, group)
    earlier = jnp.concatenate(
        [jnp.zeros((1, row_count, group), jnp.bfloat16), tap_blocks[:-1]], axis=0
    )
    segments = jnp.concatenate([earlier, tap_blocks], axis=1)
    filters = jnp.einsum(
        "fn,bnc->bcf", full_table, segments, preferred_element_type=jnp.float32
    ).astype(jnp.bfloat16)

    mixed_spec = jnp.zeros(own_spec.shape, jnp.float32)
    for lag_step in range(seq_count):
        term = spectral_product(filters[lag_step][None], own_spec[: seq_count - lag_step])
        mixed_spec = mixed_spec + jnp.pad(term, ((lag_step, 0), (0, 0), (0, 0)))
    long_cols = jnp.einsum(
        "bck,ak->abc", mixed_spec.astype(jnp.bfloat16), back_table,
        preferred_element_type=jnp.float32,
    ).astype(jnp.bfloat16)

    grad_spec = jnp.einsum(
        "abc,ak->bck", grad_long_cols, back_table, preferred_element_type=jnp.float32
    ).astype(jnp.bfloat16)
    spectral_grad = jnp.zeros(grad_spec.shape, jnp.float32)
    filter_parts = []
    for lag_step in range(seq_count):
        ahead = grad_spec[lag_step:]
        term = spectral_adjoint(filters[lag_step][None], ahead)
        spectral_grad = spectral_grad + jnp.pad(term, ((0, lag_step), (0, 0), (0, 0)))
        filter_parts.append(
            jnp.sum(spectral_adjoint(own_spec[: seq_count - lag_step], ahead), axis=0)
        )
    filter_grad = jnp.stack(filter_parts, axis=0)
    gated_grad_cols = jnp.einsum(
        "bck,kt->tbc", spectral_grad.astype(jnp.bfloat16), half_table,
        preferred_element_type=jnp.float32,
    ).astype(jnp.bfloat16)

    tap_spec = jnp.einsum("dck,kn->dcn", filter_grad, forward, precision=lax.Precision.HIGHEST)
    tap_cols = tap_spec[:, :, row_count:] + jnp.concatenate(
        [tap_spec[1:, :, :row_count], jnp.zeros((1, group, row_count), jnp.float32)], axis=0
    )
    returned = swap_layout(
        jnp.concatenate(
            [
                long_cols.astype(jnp.float32),
                gated_grad_cols.astype(jnp.float32),
                tap_cols.transpose(2, 0, 1),
            ],
            axis=2,
        )
    )
    long_out = returned[..., :group].reshape(row_count, local_width)
    gated_wide = returned[..., group : 2 * group].reshape(row_count, local_width)
    tap_grads = returned[..., 2 * group :].reshape(row_count, local_width)

    operator_out = (query_conv * long_out).astype(jnp.bfloat16)
    grad_query = cot_wide * long_out

    grad_streams = jnp.stack(
        [grad_query, gated_wide * value_conv, gated_wide * key_conv], axis=1
    ).astype(jnp.bfloat16)
    grad_streams = grad_streams.reshape(row_count, 3 * local_width)
    after = neighbour_rows(grad_streams[:2], -1)
    padded = (
        jnp.concatenate([grad_streams, after], axis=0)
        .astype(jnp.float32)
        .reshape(row_count + 2, 3, local_width)
    )
    stream_grads = (
        short_weight[:, 0] * padded[:row_count]
        + short_weight[:, 1] * padded[1 : row_count + 1]
        + short_weight[:, 2] * padded[2:]
    ).astype(jnp.bfloat16)
    return (operator_out, stream_grads, tap_grads)


def solution(mesh):
    return jax.shard_map(
        on_device,
        mesh=mesh,
        in_specs=(
            P("seq", "chan"),
            P(None, None, "chan"),
            P(None, None, "chan"),
            P(None, "chan"),
            P("seq", "chan"),
        ),
        out_specs=(P("seq", "chan"), P("seq", None, "chan"), P("seq", "chan")),
        check_vma=False,
    )
```

```python
import math

import jax
import jax.numpy as jnp
from jax import lax
from jax.sharding import PartitionSpec as P


def passed_along(block, axis, distance):
    devices = range(lax.axis_size(axis))
    route = [(i - distance, i) for i in devices if i - distance in devices]
    return lax.ppermute(block, axis, route)


def dft_tables(row_count):
    length = 2 * row_count
    sample = jnp.arange(length, dtype=jnp.int32)
    frequency = jnp.arange(row_count, dtype=jnp.int32)
    angles = (frequency[:, None] * sample[None, :] % length).astype(jnp.float32) * (
        2.0 * math.pi / length
    )
    parity = 1.0 - 2.0 * (sample % 2).astype(jnp.float32)
    lower_rows = jnp.where(frequency[:, None] == 0, parity[None, :], -jnp.sin(angles))
    forward = jnp.concatenate([jnp.cos(angles), lower_rows], axis=0)
    out_index = row_count + frequency
    back_angles = (out_index[:, None] * frequency[None, :] % length).astype(jnp.float32) * (
        2.0 * math.pi / length
    )
    factor = jnp.where(frequency == 0, 1.0, 2.0) / length
    out_parity = 1.0 - 2.0 * (out_index % 2).astype(jnp.float32)
    real_part = jnp.cos(back_angles) * factor[None, :]
    imag_part = jnp.where(
        frequency[None, :] == 0, out_parity[:, None] / length, -2.0 * jnp.sin(back_angles) / length
    )
    inverse = jnp.concatenate([real_part, imag_part], axis=1)
    return (forward, inverse)


def spectral_product(left_spec, right_spec):
    half_len = left_spec.shape[-1] // 2
    left_spec = left_spec.astype(jnp.float32)
    right_spec = right_spec.astype(jnp.float32)
    left_re, left_im = (left_spec[..., :half_len], left_spec[..., half_len:])
    right_re, right_im = (right_spec[..., :half_len], right_spec[..., half_len:])
    first_row = lax.broadcasted_iota(jnp.int32, (1,) * (left_spec.ndim - 1) + (half_len,), left_spec.ndim - 1) == 0
    cross_term = left_im * right_im
    real_out = left_re * right_re - jnp.where(first_row, 0.0, cross_term)
    imag_out = jnp.where(first_row, cross_term, left_re * right_im + left_im * right_re)
    return jnp.concatenate([real_out, imag_out], axis=-1)


def spectral_adjoint(left_spec, grad_spec):
    half_len = left_spec.shape[-1] // 2
    left_spec = left_spec.astype(jnp.float32)
    grad_spec = grad_spec.astype(jnp.float32)
    left_re, left_im = (left_spec[..., :half_len], left_spec[..., half_len:])
    grad_re, grad_im = (grad_spec[..., :half_len], grad_spec[..., half_len:])
    first_row = lax.broadcasted_iota(jnp.int32, (1,) * (left_spec.ndim - 1) + (half_len,), left_spec.ndim - 1) == 0
    cross_term = left_im * grad_im
    real_out = left_re * grad_re + jnp.where(first_row, 0.0, cross_term)
    imag_out = jnp.where(first_row, cross_term, left_re * grad_im - left_im * grad_re)
    return jnp.concatenate([real_out, imag_out], axis=-1)


def neighbour_rows(edge_rows, offset):
    return passed_along(edge_rows, "seq", offset)


def swap_layout(values):
    return lax.all_to_all(values, "seq", 1, 1, tiled=True)


def on_device(tokens, in_weight, short_weight, filter_taps, cotangent):
    row_count, local_width = tokens.shape
    seq_count = lax.axis_size("seq")
    chan_count = lax.axis_size("chan")
    group = local_width // seq_count
    own_block = lax.axis_index("seq")
    forward, inverse = dft_tables(row_count)
    full_table = forward.astype(jnp.bfloat16)
    half_table = full_table[:, :row_count]
    back_table = inverse.astype(jnp.bfloat16)

    copies = jnp.broadcast_to(tokens[None], (chan_count,) + tokens.shape)
    gathered = lax.all_to_all(copies, "chan", 0, 0, tiled=True)
    weight_parts = in_weight.reshape(chan_count, local_width, 3, local_width)
    streams = jnp.einsum(
        "stf,sfqc->tqc", gathered, weight_parts, preferred_element_type=jnp.float32
    ).astype(jnp.bfloat16)
    streams = streams.reshape(row_count, 3 * local_width)
    before = neighbour_rows(streams[row_count - 2 :], 1)
    after = neighbour_rows(jnp.concatenate([streams[:2], cotangent[:2]], axis=1), -1)
    next_streams, next_cot = (after[:, : 3 * local_width], after[:, 3 * local_width :])
    extended = (
        jnp.concatenate([before, streams, next_streams], axis=0)
        .astype(jnp.float32)
        .reshape(row_count + 4, 3, local_width)
    )
    conv_out = (
        short_weight[:, 0] * extended[2:]
        + short_weight[:, 1] * extended[1:-1]
        + short_weight[:, 2] * extended[:-2]
    )
    query_conv, key_conv, value_conv = (conv_out[:, 0], conv_out[:, 1], conv_out[:, 2])
    gated = (key_conv[:row_count] * value_conv[:row_count]).astype(jnp.bfloat16)
    cot_wide = jnp.concatenate([cotangent, next_cot], axis=0).astype(jnp.float32)
    grad_long = (cot_wide[:row_count] * query_conv[:row_count]).astype(jnp.bfloat16)

    both_cols = swap_layout(
        jnp.concatenate(
            [gated.reshape(row_count, seq_count, group), grad_long.reshape(row_count, seq_count, group)],
            axis=2,
        )
    )
    gated_cols, grad_long_cols = (both_cols[..., :group], both_cols[..., group:])
    own_spec = jnp.einsum(
        "tbc,kt->bck", gated_cols, half_table, preferred_element_type=jnp.float32
    ).astype(jnp.bfloat16)
    own_taps = lax.dynamic_slice_in_dim(filter_taps, own_block * group, group, axis=1)
    tap_blocks = own_taps.reshape(seq_count, row_count, group)
    earlier = jnp.concatenate(
        [jnp.zeros((1, row_count, group), jnp.bfloat16), tap_blocks[:-1]], axis=0
    )
    segments = jnp.concatenate([earlier, tap_blocks], axis=1)
    filters = jnp.einsum(
        "fn,bnc->bcf", full_table, segments, preferred_element_type=jnp.float32
    ).astype(jnp.bfloat16)

    mixed_spec = jnp.zeros(own_spec.shape, jnp.float32)
    for lag_step in range(seq_count):
        term = spectral_product(filters[lag_step][None], own_spec[: seq_count - lag_step])
        mixed_spec = mixed_spec + jnp.pad(term, ((lag_step, 0), (0, 0), (0, 0)))
    long_cols = jnp.einsum(
        "bck,ak->abc", mixed_spec.astype(jnp.bfloat16), back_table,
        preferred_element_type=jnp.float32,
    ).astype(jnp.bfloat16)

    grad_spec = jnp.einsum(
        "abc,ak->bck", grad_long_cols, back_table, preferred_element_type=jnp.float32
    ).astype(jnp.bfloat16)
    spectral_grad = jnp.zeros(grad_spec.shape, jnp.float32)
    filter_parts = []
    for lag_step in range(seq_count):
        ahead = grad_spec[lag_step:]
        term = spectral_adjoint(filters[lag_step][None], ahead)
        spectral_grad = spectral_grad + jnp.pad(term, ((0, lag_step), (0, 0), (0, 0)))
        filter_parts.append(
            jnp.sum(spectral_adjoint(own_spec[: seq_count - lag_step], ahead), axis=0)
        )
    filter_grad = jnp.stack(filter_parts, axis=0)
    gated_grad_cols = jnp.einsum(
        "bck,kt->tbc", spectral_grad.astype(jnp.bfloat16), half_table,
        preferred_element_type=jnp.float32,
    ).astype(jnp.bfloat16)

    tap_spec = jnp.einsum("dck,kn->dcn", filter_grad, forward, precision=lax.Precision.HIGHEST)
    tap_cols = tap_spec[:, :, row_count:] + jnp.concatenate(
        [tap_spec[1:, :, :row_count], jnp.zeros((1, group, row_count), jnp.float32)], axis=0
    )
    tap_cols = tap_cols.transpose(2, 0, 1).astype(jnp.bfloat16)

    def with_next_rows(cols):
        following = jnp.concatenate(
            [cols[:2, 1:], jnp.zeros((2, 1, group), cols.dtype)], axis=1
        )
        return jnp.concatenate([cols, following], axis=0)

    returned = swap_layout(
        jnp.concatenate(
            [
                with_next_rows(long_cols),
                with_next_rows(gated_grad_cols),
                jnp.concatenate([tap_cols, jnp.zeros((2, seq_count, group), jnp.bfloat16)], axis=0),
            ],
            axis=2,
        )
    )
    wide_rows = row_count + 2
    long_out = returned[..., :group].reshape(wide_rows, local_width).astype(jnp.float32)
    gated_wide = returned[..., group : 2 * group].reshape(wide_rows, local_width).astype(jnp.float32)
    tap_grads = returned[:row_count, :, 2 * group :].astype(jnp.float32).reshape(row_count, local_width)

    operator_out = (query_conv[:row_count] * long_out[:row_count]).astype(jnp.bfloat16)
    grad_query = cot_wide * long_out
    grad_streams = jnp.stack(
        [grad_query, gated_wide * value_conv, gated_wide * key_conv], axis=1
    ).astype(jnp.bfloat16).astype(jnp.float32)
    stream_grads = (
        short_weight[:, 0] * grad_streams[:row_count]
        + short_weight[:, 1] * grad_streams[1 : row_count + 1]
        + short_weight[:, 2] * grad_streams[2:]
    ).astype(jnp.bfloat16)
    return (operator_out, stream_grads, tap_grads)


def solution(mesh):
    return jax.shard_map(
        on_device,
        mesh=mesh,
        in_specs=(
            P("seq", "chan"),
            P(None, None, "chan"),
            P(None, None, "chan"),
            P(None, "chan"),
            P("seq", "chan"),
        ),
        out_specs=(P("seq", "chan"), P("seq", None, "chan"), P("seq", "chan")),
        check_vma=False,
    )
```

```python
import math

import jax
import jax.numpy as jnp
from jax import lax
from jax.sharding import PartitionSpec as P


def passed_along(block, axis, distance):
    devices = range(lax.axis_size(axis))
    route = [(i - distance, i) for i in devices if i - distance in devices]
    return lax.ppermute(block, axis, route)


def dft_tables(row_count):
    length = 2 * row_count
    sample = jnp.arange(length, dtype=jnp.int32)
    frequency = jnp.arange(row_count, dtype=jnp.int32)
    angles = (frequency[:, None] * sample[None, :] % length).astype(jnp.float32) * (
        2.0 * math.pi / length
    )
    parity = 1.0 - 2.0 * (sample % 2).astype(jnp.float32)
    lower_rows = jnp.where(frequency[:, None] == 0, parity[None, :], -jnp.sin(angles))
    forward = jnp.concatenate([jnp.cos(angles), lower_rows], axis=0)
    out_index = row_count + frequency
    back_angles = (out_index[:, None] * frequency[None, :] % length).astype(jnp.float32) * (
        2.0 * math.pi / length
    )
    factor = jnp.where(frequency == 0, 1.0, 2.0) / length
    out_parity = 1.0 - 2.0 * (out_index % 2).astype(jnp.float32)
    real_part = jnp.cos(back_angles) * factor[None, :]
    imag_part = jnp.where(
        frequency[None, :] == 0, out_parity[:, None] / length, -2.0 * jnp.sin(back_angles) / length
    )
    inverse = jnp.concatenate([real_part, imag_part], axis=1)
    return (forward, inverse)


def spectral_product(left_spec, right_spec):
    half_len = left_spec.shape[-1] // 2
    left_spec = left_spec.astype(jnp.float32)
    right_spec = right_spec.astype(jnp.float32)
    left_re, left_im = (left_spec[..., :half_len], left_spec[..., half_len:])
    right_re, right_im = (right_spec[..., :half_len], right_spec[..., half_len:])
    first_row = lax.broadcasted_iota(jnp.int32, (1,) * (left_spec.ndim - 1) + (half_len,), left_spec.ndim - 1) == 0
    cross_term = left_im * right_im
    real_out = left_re * right_re - jnp.where(first_row, 0.0, cross_term)
    imag_out = jnp.where(first_row, cross_term, left_re * right_im + left_im * right_re)
    return jnp.concatenate([real_out, imag_out], axis=-1)


def spectral_adjoint(left_spec, grad_spec):
    half_len = left_spec.shape[-1] // 2
    left_spec = left_spec.astype(jnp.float32)
    grad_spec = grad_spec.astype(jnp.float32)
    left_re, left_im = (left_spec[..., :half_len], left_spec[..., half_len:])
    grad_re, grad_im = (grad_spec[..., :half_len], grad_spec[..., half_len:])
    first_row = lax.broadcasted_iota(jnp.int32, (1,) * (left_spec.ndim - 1) + (half_len,), left_spec.ndim - 1) == 0
    cross_term = left_im * grad_im
    real_out = left_re * grad_re + jnp.where(first_row, 0.0, cross_term)
    imag_out = jnp.where(first_row, cross_term, left_re * grad_im - left_im * grad_re)
    return jnp.concatenate([real_out, imag_out], axis=-1)


def neighbour_rows(edge_rows, offset):
    return passed_along(edge_rows, "seq", offset)


def swap_layout(values):
    return lax.all_to_all(values, "seq", 1, 1, tiled=True)


def on_device(tokens, in_weight, short_weight, filter_taps, cotangent):
    row_count, local_width = tokens.shape
    seq_count = lax.axis_size("seq")
    chan_count = lax.axis_size("chan")
    group = local_width // seq_count
    own_block = lax.axis_index("seq")
    forward, inverse = dft_tables(row_count)
    full_table = forward.astype(jnp.bfloat16)
    half_table = full_table[:, :row_count]
    back_table = inverse.astype(jnp.bfloat16)

    copies = jnp.broadcast_to(tokens[None], (chan_count,) + tokens.shape)
    gathered = lax.all_to_all(copies, "chan", 0, 0, tiled=True)
    weight_parts = in_weight.reshape(chan_count, local_width, 3, local_width)
    streams = jnp.einsum(
        "stf,sfqc->qtc", gathered, weight_parts, preferred_element_type=jnp.float32
    ).astype(jnp.bfloat16)
    before = neighbour_rows(streams[:, row_count - 2 :], 1)
    after = neighbour_rows(jnp.concatenate([streams[:, :2], cotangent[None, :2]], axis=0), -1)
    next_streams, next_cot = (after[:3], after[3])
    extended = jnp.concatenate([before, streams, next_streams], axis=1).astype(jnp.float32)
    conv_weight = short_weight[:, :, None, :]
    conv_out = (
        conv_weight[:, 0] * extended[:, 2:]
        + conv_weight[:, 1] * extended[:, 1:-1]
        + conv_weight[:, 2] * extended[:, :-2]
    )
    query_conv, key_conv, value_conv = (conv_out[0], conv_out[1], conv_out[2])
    gated = (key_conv[:row_count] * value_conv[:row_count]).astype(jnp.bfloat16)
    cot_wide = jnp.concatenate([cotangent, next_cot], axis=0).astype(jnp.float32)
    grad_long = (cot_wide[:row_count] * query_conv[:row_count]).astype(jnp.bfloat16)

    both_cols = swap_layout(
        jnp.concatenate(
            [gated.reshape(row_count, seq_count, group), grad_long.reshape(row_count, seq_count, group)],
            axis=2,
        )
    )
    gated_cols, grad_long_cols = (both_cols[..., :group], both_cols[..., group:])
    own_spec = jnp.einsum(
        "tbc,kt->bck", gated_cols, half_table, preferred_element_type=jnp.float32
    ).astype(jnp.bfloat16)
    own_taps = lax.dynamic_slice_in_dim(filter_taps, own_block * group, group, axis=1)
    tap_blocks = own_taps.reshape(seq_count, row_count, group)
    earlier = jnp.concatenate(
        [jnp.zeros((1, row_count, group), jnp.bfloat16), tap_blocks[:-1]], axis=0
    )
    segments = jnp.concatenate([earlier, tap_blocks], axis=1)
    filters = jnp.einsum(
        "fn,bnc->bcf", full_table, segments, preferred_element_type=jnp.float32
    ).astype(jnp.bfloat16)

    mixed_spec = jnp.zeros(own_spec.shape, jnp.float32)
    for lag_step in range(seq_count):
        term = spectral_product(filters[lag_step][None], own_spec[: seq_count - lag_step])
        mixed_spec = mixed_spec + jnp.pad(term, ((lag_step, 0), (0, 0), (0, 0)))
    long_cols = jnp.einsum(
        "bck,ak->abc", mixed_spec.astype(jnp.bfloat16), back_table,
        preferred_element_type=jnp.float32,
    ).astype(jnp.bfloat16)

    grad_spec = jnp.einsum(
        "abc,ak->bck", grad_long_cols, back_table, preferred_element_type=jnp.float32
    ).astype(jnp.bfloat16)
    spectral_grad = jnp.zeros(grad_spec.shape, jnp.float32)
    filter_parts = []
    for lag_step in range(seq_count):
        ahead = grad_spec[lag_step:]
        term = spectral_adjoint(filters[lag_step][None], ahead)
        spectral_grad = spectral_grad + jnp.pad(term, ((0, lag_step), (0, 0), (0, 0)))
        filter_parts.append(
            jnp.sum(spectral_adjoint(own_spec[: seq_count - lag_step], ahead), axis=0)
        )
    filter_grad = jnp.stack(filter_parts, axis=0)
    gated_grad_cols = jnp.einsum(
        "bck,kt->tbc", spectral_grad.astype(jnp.bfloat16), half_table,
        preferred_element_type=jnp.float32,
    ).astype(jnp.bfloat16)

    tap_spec = jnp.einsum("dck,kn->dcn", filter_grad, forward, precision=lax.Precision.HIGHEST)
    tap_cols = tap_spec[:, :, row_count:] + jnp.concatenate(
        [tap_spec[1:, :, :row_count], jnp.zeros((1, group, row_count), jnp.float32)], axis=0
    )
    tap_cols = tap_cols.transpose(2, 0, 1).astype(jnp.bfloat16)

    def with_next_rows(cols):
        following = jnp.concatenate(
            [cols[:2, 1:], jnp.zeros((2, 1, group), cols.dtype)], axis=1
        )
        return jnp.concatenate([cols, following], axis=0)

    returned = swap_layout(
        jnp.concatenate(
            [
                with_next_rows(long_cols),
                with_next_rows(gated_grad_cols),
                jnp.concatenate([tap_cols, jnp.zeros((2, seq_count, group), jnp.bfloat16)], axis=0),
            ],
            axis=2,
        )
    )
    wide_rows = row_count + 2
    long_out = returned[..., :group].reshape(wide_rows, local_width).astype(jnp.float32)
    gated_wide = returned[..., group : 2 * group].reshape(wide_rows, local_width).astype(jnp.float32)
    tap_grads = returned[:row_count, :, 2 * group :].astype(jnp.float32).reshape(row_count, local_width)

    operator_out = (query_conv[:row_count] * long_out[:row_count]).astype(jnp.bfloat16)
    grad_query = cot_wide * long_out
    grad_streams = jnp.stack(
        [grad_query, gated_wide * value_conv, gated_wide * key_conv], axis=0
    ).astype(jnp.bfloat16).astype(jnp.float32)
    stream_grads = (
        conv_weight[:, 0] * grad_streams[:, :row_count]
        + conv_weight[:, 1] * grad_streams[:, 1 : row_count + 1]
        + conv_weight[:, 2] * grad_streams[:, 2:]
    ).astype(jnp.bfloat16).transpose(1, 0, 2)
    return (operator_out, stream_grads, tap_grads)


def solution(mesh):
    return jax.shard_map(
        on_device,
        mesh=mesh,
        in_specs=(
            P("seq", "chan"),
            P(None, None, "chan"),
            P(None, None, "chan"),
            P(None, "chan"),
            P("seq", "chan"),
        ),
        out_specs=(P("seq", "chan"), P("seq", None, "chan"), P("seq", "chan")),
        check_vma=False,
    )
```

```python
import math

import jax
import jax.numpy as jnp
from jax import lax
from jax.sharding import PartitionSpec as P


def passed_along(block, axis, distance):
    devices = range(lax.axis_size(axis))
    route = [(i - distance, i) for i in devices if i - distance in devices]
    return lax.ppermute(block, axis, route)


def dft_tables(row_count):
    length = 2 * row_count
    sample = jnp.arange(length, dtype=jnp.int32)
    frequency = jnp.arange(row_count, dtype=jnp.int32)
    angles = (frequency[:, None] * sample[None, :] % length).astype(jnp.float32) * (
        2.0 * math.pi / length
    )
    parity = 1.0 - 2.0 * (sample % 2).astype(jnp.float32)
    lower_rows = jnp.where(frequency[:, None] == 0, parity[None, :], -jnp.sin(angles))
    forward = jnp.concatenate([jnp.cos(angles), lower_rows], axis=0)
    out_index = row_count + frequency
    back_angles = (out_index[:, None] * frequency[None, :] % length).astype(jnp.float32) * (
        2.0 * math.pi / length
    )
    factor = jnp.where(frequency == 0, 1.0, 2.0) / length
    out_parity = 1.0 - 2.0 * (out_index % 2).astype(jnp.float32)
    real_part = jnp.cos(back_angles) * factor[None, :]
    imag_part = jnp.where(
        frequency[None, :] == 0, out_parity[:, None] / length, -2.0 * jnp.sin(back_angles) / length
    )
    inverse = jnp.concatenate([real_part, imag_part], axis=1)
    return (forward, inverse)


def spectral_product(left_spec, right_spec):
    half_len = left_spec.shape[-1] // 2
    left_spec = left_spec.astype(jnp.float32)
    right_spec = right_spec.astype(jnp.float32)
    left_re, left_im = (left_spec[..., :half_len], left_spec[..., half_len:])
    right_re, right_im = (right_spec[..., :half_len], right_spec[..., half_len:])
    first_row = lax.broadcasted_iota(jnp.int32, (1,) * (left_spec.ndim - 1) + (half_len,), left_spec.ndim - 1) == 0
    cross_term = left_im * right_im
    real_out = left_re * right_re - jnp.where(first_row, 0.0, cross_term)
    imag_out = jnp.where(first_row, cross_term, left_re * right_im + left_im * right_re)
    return jnp.concatenate([real_out, imag_out], axis=-1)


def spectral_adjoint(left_spec, grad_spec):
    half_len = left_spec.shape[-1] // 2
    left_spec = left_spec.astype(jnp.float32)
    grad_spec = grad_spec.astype(jnp.float32)
    left_re, left_im = (left_spec[..., :half_len], left_spec[..., half_len:])
    grad_re, grad_im = (grad_spec[..., :half_len], grad_spec[..., half_len:])
    first_row = lax.broadcasted_iota(jnp.int32, (1,) * (left_spec.ndim - 1) + (half_len,), left_spec.ndim - 1) == 0
    cross_term = left_im * grad_im
    real_out = left_re * grad_re + jnp.where(first_row, 0.0, cross_term)
    imag_out = jnp.where(first_row, cross_term, left_re * grad_im - left_im * grad_re)
    return jnp.concatenate([real_out, imag_out], axis=-1)


def neighbour_rows(edge_rows, offset):
    return passed_along(edge_rows, "seq", offset)


def swap_layout(values):
    return lax.all_to_all(values, "seq", 1, 1, tiled=True)


def on_device(tokens, in_weight, short_weight, filter_taps, cotangent):
    row_count, local_width = tokens.shape
    seq_count = lax.axis_size("seq")
    chan_count = lax.axis_size("chan")
    group = local_width // seq_count
    own_block = lax.axis_index("seq")
    forward, inverse = dft_tables(row_count)
    full_table = forward.astype(jnp.bfloat16)
    half_table = full_table[:, :row_count]
    back_table = inverse.astype(jnp.bfloat16)

    copies = jnp.broadcast_to(tokens[None], (chan_count,) + tokens.shape)
    gathered = lax.all_to_all(copies, "chan", 0, 0, tiled=True)
    weight_parts = in_weight.reshape(chan_count, local_width, 3, local_width)
    streams = jnp.einsum(
        "stf,sfqc->qtc", gathered, weight_parts, preferred_element_type=jnp.float32
    ).astype(jnp.bfloat16)
    before = neighbour_rows(streams[:, row_count - 2 :], 1)
    extended = jnp.concatenate([before, streams], axis=1).astype(jnp.float32)
    conv_weight = short_weight[:, :, None, :]
    conv_out = (
        conv_weight[:, 0] * extended[:, 2:]
        + conv_weight[:, 1] * extended[:, 1:-1]
        + conv_weight[:, 2] * extended[:, :-2]
    )
    query_conv, key_conv, value_conv = (conv_out[0], conv_out[1], conv_out[2])
    gated = (key_conv * value_conv).astype(jnp.bfloat16)
    grad_long = (cotangent.astype(jnp.float32) * query_conv).astype(jnp.bfloat16)

    both_cols = swap_layout(
        jnp.concatenate(
            [gated.reshape(row_count, seq_count, group), grad_long.reshape(row_count, seq_count, group)],
            axis=2,
        )
    )
    gated_cols, grad_long_cols = (both_cols[..., :group], both_cols[..., group:])

    after_rows, _ = lax.optimization_barrier(
        (jnp.concatenate([streams[:, :2], cotangent[None, :2]], axis=0), both_cols)
    )
    after = neighbour_rows(after_rows, -1)
    next_streams, next_cot = (after[:3], after[3])
    edge = jnp.concatenate([streams[:, row_count - 2 :], next_streams], axis=1).astype(jnp.float32)
    edge_out = (
        conv_weight[:, 0] * edge[:, 2:]
        + conv_weight[:, 1] * edge[:, 1:-1]
        + conv_weight[:, 2] * edge[:, :-2]
    )
    query_conv = jnp.concatenate([query_conv, edge_out[0]], axis=0)
    key_conv = jnp.concatenate([key_conv, edge_out[1]], axis=0)
    value_conv = jnp.concatenate([value_conv, edge_out[2]], axis=0)
    cot_wide = jnp.concatenate([cotangent, next_cot], axis=0).astype(jnp.float32)
    own_spec = jnp.einsum(
        "tbc,kt->bck", gated_cols, half_table, preferred_element_type=jnp.float32
    ).astype(jnp.bfloat16)
    own_taps = lax.dynamic_slice_in_dim(filter_taps, own_block * group, group, axis=1)
    tap_blocks = own_taps.reshape(seq_count, row_count, group)
    earlier = jnp.concatenate(
        [jnp.zeros((1, row_count, group), jnp.bfloat16), tap_blocks[:-1]], axis=0
    )
    segments = jnp.concatenate([earlier, tap_blocks], axis=1)
    filters = jnp.einsum(
        "fn,bnc->bcf", full_table, segments, preferred_element_type=jnp.float32
    ).astype(jnp.bfloat16)

    mixed_spec = jnp.zeros(own_spec.shape, jnp.float32)
    for lag_step in range(seq_count):
        term = spectral_product(filters[lag_step][None], own_spec[: seq_count - lag_step])
        mixed_spec = mixed_spec + jnp.pad(term, ((lag_step, 0), (0, 0), (0, 0)))
    long_cols = jnp.einsum(
        "bck,ak->abc", mixed_spec.astype(jnp.bfloat16), back_table,
        preferred_element_type=jnp.float32,
    ).astype(jnp.bfloat16)

    grad_spec = jnp.einsum(
        "abc,ak->bck", grad_long_cols, back_table, preferred_element_type=jnp.float32
    ).astype(jnp.bfloat16)
    spectral_grad = jnp.zeros(grad_spec.shape, jnp.float32)
    filter_parts = []
    for lag_step in range(seq_count):
        ahead = grad_spec[lag_step:]
        term = spectral_adjoint(filters[lag_step][None], ahead)
        spectral_grad = spectral_grad + jnp.pad(term, ((0, lag_step), (0, 0), (0, 0)))
        filter_parts.append(
            jnp.sum(spectral_adjoint(own_spec[: seq_count - lag_step], ahead), axis=0)
        )
    filter_grad = jnp.stack(filter_parts, axis=0)
    gated_grad_cols = jnp.einsum(
        "bck,kt->tbc", spectral_grad.astype(jnp.bfloat16), half_table,
        preferred_element_type=jnp.float32,
    ).astype(jnp.bfloat16)

    tap_spec = jnp.einsum("dck,kn->dcn", filter_grad, forward, precision=lax.Precision.HIGHEST)
    tap_cols = tap_spec[:, :, row_count:] + jnp.concatenate(
        [tap_spec[1:, :, :row_count], jnp.zeros((1, group, row_count), jnp.float32)], axis=0
    )
    tap_cols = tap_cols.transpose(2, 0, 1).astype(jnp.bfloat16)

    def with_next_rows(cols):
        following = jnp.concatenate(
            [cols[:2, 1:], jnp.zeros((2, 1, group), cols.dtype)], axis=1
        )
        return jnp.concatenate([cols, following], axis=0)

    returned = swap_layout(
        jnp.concatenate(
            [
                with_next_rows(long_cols),
                with_next_rows(gated_grad_cols),
                jnp.concatenate([tap_cols, jnp.zeros((2, seq_count, group), jnp.bfloat16)], axis=0),
            ],
            axis=2,
        )
    )
    wide_rows = row_count + 2
    long_out = returned[..., :group].reshape(wide_rows, local_width).astype(jnp.float32)
    gated_wide = returned[..., group : 2 * group].reshape(wide_rows, local_width).astype(jnp.float32)
    tap_grads = returned[:row_count, :, 2 * group :].astype(jnp.float32).reshape(row_count, local_width)

    operator_out = (query_conv[:row_count] * long_out[:row_count]).astype(jnp.bfloat16)
    grad_query = cot_wide * long_out
    grad_streams = jnp.stack(
        [grad_query, gated_wide * value_conv, gated_wide * key_conv], axis=0
    ).astype(jnp.bfloat16).astype(jnp.float32)
    stream_grads = (
        conv_weight[:, 0] * grad_streams[:, :row_count]
        + conv_weight[:, 1] * grad_streams[:, 1 : row_count + 1]
        + conv_weight[:, 2] * grad_streams[:, 2:]
    ).astype(jnp.bfloat16).transpose(1, 0, 2)
    return (operator_out, stream_grads, tap_grads)


def solution(mesh):
    return jax.shard_map(
        on_device,
        mesh=mesh,
        in_specs=(
            P("seq", "chan"),
            P(None, None, "chan"),
            P(None, None, "chan"),
            P(None, "chan"),
            P("seq", "chan"),
        ),
        out_specs=(P("seq", "chan"), P("seq", None, "chan"), P("seq", "chan")),
        check_vma=False,
    )
```

```python
import math

import jax
import jax.numpy as jnp
from jax import lax
from jax.sharding import PartitionSpec as P


def passed_along(block, axis, distance):
    devices = range(lax.axis_size(axis))
    route = [(i - distance, i) for i in devices if i - distance in devices]
    return lax.ppermute(block, axis, route)


def dft_tables(row_count):
    length = 2 * row_count
    sample = jnp.arange(length, dtype=jnp.int32)
    frequency = jnp.arange(row_count, dtype=jnp.int32)
    angles = (frequency[:, None] * sample[None, :] % length).astype(jnp.float32) * (
        2.0 * math.pi / length
    )
    parity = 1.0 - 2.0 * (sample % 2).astype(jnp.float32)
    lower_rows = jnp.where(frequency[:, None] == 0, parity[None, :], -jnp.sin(angles))
    forward = jnp.concatenate([jnp.cos(angles), lower_rows], axis=0)
    out_index = row_count + frequency
    back_angles = (out_index[:, None] * frequency[None, :] % length).astype(jnp.float32) * (
        2.0 * math.pi / length
    )
    factor = jnp.where(frequency == 0, 1.0, 2.0) / length
    out_parity = 1.0 - 2.0 * (out_index % 2).astype(jnp.float32)
    real_part = jnp.cos(back_angles) * factor[None, :]
    imag_part = jnp.where(
        frequency[None, :] == 0, out_parity[:, None] / length, -2.0 * jnp.sin(back_angles) / length
    )
    inverse = jnp.concatenate([real_part, imag_part], axis=1)
    return (forward, inverse)


def spectral_product(left_spec, right_spec):
    half_len = left_spec.shape[-1] // 2
    left_spec = left_spec.astype(jnp.float32)
    right_spec = right_spec.astype(jnp.float32)
    left_re, left_im = (left_spec[..., :half_len], left_spec[..., half_len:])
    right_re, right_im = (right_spec[..., :half_len], right_spec[..., half_len:])
    first_row = lax.broadcasted_iota(jnp.int32, (1,) * (left_spec.ndim - 1) + (half_len,), left_spec.ndim - 1) == 0
    cross_term = left_im * right_im
    real_out = left_re * right_re - jnp.where(first_row, 0.0, cross_term)
    imag_out = jnp.where(first_row, cross_term, left_re * right_im + left_im * right_re)
    return jnp.concatenate([real_out, imag_out], axis=-1)


def spectral_adjoint(left_spec, grad_spec):
    half_len = left_spec.shape[-1] // 2
    left_spec = left_spec.astype(jnp.float32)
    grad_spec = grad_spec.astype(jnp.float32)
    left_re, left_im = (left_spec[..., :half_len], left_spec[..., half_len:])
    grad_re, grad_im = (grad_spec[..., :half_len], grad_spec[..., half_len:])
    first_row = lax.broadcasted_iota(jnp.int32, (1,) * (left_spec.ndim - 1) + (half_len,), left_spec.ndim - 1) == 0
    cross_term = left_im * grad_im
    real_out = left_re * grad_re + jnp.where(first_row, 0.0, cross_term)
    imag_out = jnp.where(first_row, cross_term, left_re * grad_im - left_im * grad_re)
    return jnp.concatenate([real_out, imag_out], axis=-1)


def neighbour_rows(edge_rows, offset):
    return passed_along(edge_rows, "seq", offset)


def swap_layout(values):
    return lax.all_to_all(values, "seq", 1, 1, tiled=True)


def on_device(tokens, in_weight, short_weight, filter_taps, cotangent):
    row_count, local_width = tokens.shape
    seq_count = lax.axis_size("seq")
    chan_count = lax.axis_size("chan")
    group = local_width // seq_count
    own_block = lax.axis_index("seq")
    forward, inverse = dft_tables(row_count)
    full_table = forward.astype(jnp.bfloat16)
    half_table = full_table[:, :row_count]
    back_table = inverse.astype(jnp.bfloat16)

    copies = jnp.broadcast_to(tokens[None], (chan_count,) + tokens.shape)
    gathered = lax.all_to_all(copies, "chan", 0, 0, tiled=True)
    weight_parts = in_weight.reshape(chan_count, local_width, 3, local_width)
    streams = jnp.einsum(
        "stf,sfqc->qtc", gathered, weight_parts, preferred_element_type=jnp.float32
    ).astype(jnp.bfloat16)
    conv_weight = short_weight[:, :, None, :]

    def short_conv(rows):
        return (
            conv_weight[:, 0] * rows[:, 2:]
            + conv_weight[:, 1] * rows[:, 1:-1]
            + conv_weight[:, 2] * rows[:, :-2]
        )

    lead = jnp.zeros((3, 2, local_width), jnp.bfloat16)
    conv_out = short_conv(jnp.concatenate([lead, streams], axis=1).astype(jnp.float32))
    query_conv, key_conv, value_conv = (conv_out[0], conv_out[1], conv_out[2])
    gated = (key_conv * value_conv).astype(jnp.bfloat16)
    grad_long = (cotangent.astype(jnp.float32) * query_conv).astype(jnp.bfloat16)
    edge_rows = jnp.concatenate([streams[:, :2], streams[:, row_count - 2 :]], axis=1)
    edge_rows = edge_rows.reshape(12, local_width)
    plane_a = jnp.concatenate([gated, edge_rows], axis=0)
    plane_b = jnp.concatenate(
        [grad_long, cotangent[:2], jnp.zeros((10, local_width), jnp.bfloat16)], axis=0
    )
    wide_in = row_count + 12

    both_cols = swap_layout(
        jnp.concatenate(
            [plane_a.reshape(wide_in, seq_count, group), plane_b.reshape(wide_in, seq_count, group)],
            axis=2,
        )
    )
    own_weight = lax.dynamic_slice_in_dim(short_weight, own_block * group, group, axis=2)
    edge_cols = both_cols[row_count:, :, :group].reshape(3, 4, seq_count, group).astype(jnp.float32)
    first, second = (edge_cols[:, 0], edge_cols[:, 1])
    zero_block = jnp.zeros((3, 1, group), jnp.float32)
    last_but_one = jnp.concatenate([zero_block, edge_cols[:, 2, :-1]], axis=1)
    last = jnp.concatenate([zero_block, edge_cols[:, 3, :-1]], axis=1)
    cols_weight = own_weight[:, :, None, :]
    head0 = cols_weight[:, 0] * first + cols_weight[:, 1] * last + cols_weight[:, 2] * last_but_one
    head1 = cols_weight[:, 0] * second + cols_weight[:, 1] * first + cols_weight[:, 2] * last
    head = jnp.stack([head0, head1], axis=1)
    head_cot = both_cols[row_count : row_count + 2, :, group:].astype(jnp.float32)
    gated_cols = jnp.concatenate(
        [(head[1] * head[2]).astype(jnp.bfloat16), both_cols[2:row_count, :, :group]], axis=0
    )
    grad_long_cols = jnp.concatenate(
        [(head_cot * head[0]).astype(jnp.bfloat16), both_cols[2:row_count, :, group:]], axis=0
    )

    edge_send, _ = lax.optimization_barrier(
        ((streams[:, row_count - 2 :], jnp.concatenate([streams[:, :2], cotangent[None, :2]], axis=0)), both_cols)
    )
    before = neighbour_rows(edge_send[0], 1)
    after = neighbour_rows(edge_send[1], -1)
    next_streams, next_cot = (after[:3], after[3])
    fixed = short_conv(jnp.concatenate([before, streams[:, :2]], axis=1).astype(jnp.float32))
    edge_out = short_conv(
        jnp.concatenate([streams[:, row_count - 2 :], next_streams], axis=1).astype(jnp.float32)
    )
    query_conv = jnp.concatenate([fixed[0], query_conv[2:], edge_out[0]], axis=0)
    key_conv = jnp.concatenate([fixed[1], key_conv[2:], edge_out[1]], axis=0)
    value_conv = jnp.concatenate([fixed[2], value_conv[2:], edge_out[2]], axis=0)
    cot_wide = jnp.concatenate([cotangent, next_cot], axis=0).astype(jnp.float32)

    own_spec = jnp.einsum(
        "tbc,kt->bck", gated_cols, half_table, preferred_element_type=jnp.float32
    ).astype(jnp.bfloat16)
    own_taps = lax.dynamic_slice_in_dim(filter_taps, own_block * group, group, axis=1)
    tap_blocks = own_taps.reshape(seq_count, row_count, group)
    earlier = jnp.concatenate(
        [jnp.zeros((1, row_count, group), jnp.bfloat16), tap_blocks[:-1]], axis=0
    )
    segments = jnp.concatenate([earlier, tap_blocks], axis=1)
    filters = jnp.einsum(
        "fn,bnc->bcf", full_table, segments, preferred_element_type=jnp.float32
    ).astype(jnp.bfloat16)

    mixed_spec = jnp.zeros(own_spec.shape, jnp.float32)
    for lag_step in range(seq_count):
        term = spectral_product(filters[lag_step][None], own_spec[: seq_count - lag_step])
        mixed_spec = mixed_spec + jnp.pad(term, ((lag_step, 0), (0, 0), (0, 0)))
    long_cols = jnp.einsum(
        "bck,ak->abc", mixed_spec.astype(jnp.bfloat16), back_table,
        preferred_element_type=jnp.float32,
    ).astype(jnp.bfloat16)

    grad_spec = jnp.einsum(
        "abc,ak->bck", grad_long_cols, back_table, preferred_element_type=jnp.float32
    ).astype(jnp.bfloat16)
    spectral_grad = jnp.zeros(grad_spec.shape, jnp.float32)
    filter_parts = []
    for lag_step in range(seq_count):
        ahead = grad_spec[lag_step:]
        term = spectral_adjoint(filters[lag_step][None], ahead)
        spectral_grad = spectral_grad + jnp.pad(term, ((0, lag_step), (0, 0), (0, 0)))
        filter_parts.append(
            jnp.sum(spectral_adjoint(own_spec[: seq_count - lag_step], ahead), axis=0)
        )
    filter_grad = jnp.stack(filter_parts, axis=0)
    gated_grad_cols = jnp.einsum(
        "bck,kt->tbc", spectral_grad.astype(jnp.bfloat16), half_table,
        preferred_element_type=jnp.float32,
    ).astype(jnp.bfloat16)

    tap_spec = jnp.einsum("dck,kn->dcn", filter_grad, forward, precision=lax.Precision.HIGHEST)
    tap_cols = tap_spec[:, :, row_count:] + jnp.concatenate(
        [tap_spec[1:, :, :row_count], jnp.zeros((1, group, row_count), jnp.float32)], axis=0
    )
    tap_cols = tap_cols.transpose(2, 0, 1).astype(jnp.bfloat16)

    def with_next_rows(cols):
        following = jnp.concatenate(
            [cols[:2, 1:], jnp.zeros((2, 1, group), cols.dtype)], axis=1
        )
        return jnp.concatenate([cols, following], axis=0)

    returned = swap_layout(
        jnp.concatenate(
            [
                with_next_rows(long_cols),
                with_next_rows(gated_grad_cols),
                jnp.concatenate([tap_cols, jnp.zeros((2, seq_count, group), jnp.bfloat16)], axis=0),
            ],
            axis=2,
        )
    )
    wide_rows = row_count + 2
    long_out = returned[..., :group].reshape(wide_rows, local_width).astype(jnp.float32)
    gated_wide = returned[..., group : 2 * group].reshape(wide_rows, local_width).astype(jnp.float32)
    tap_grads = returned[:row_count, :, 2 * group :].astype(jnp.float32).reshape(row_count, local_width)

    operator_out = (query_conv[:row_count] * long_out[:row_count]).astype(jnp.bfloat16)
    grad_query = cot_wide * long_out
    grad_streams = jnp.stack(
        [grad_query, gated_wide * value_conv, gated_wide * key_conv], axis=0
    ).astype(jnp.bfloat16).astype(jnp.float32)
    stream_grads = (
        conv_weight[:, 0] * grad_streams[:, :row_count]
        + conv_weight[:, 1] * grad_streams[:, 1 : row_count + 1]
        + conv_weight[:, 2] * grad_streams[:, 2:]
    ).astype(jnp.bfloat16).transpose(1, 0, 2)
    return (operator_out, stream_grads, tap_grads)


def solution(mesh):
    return jax.shard_map(
        on_device,
        mesh=mesh,
        in_specs=(
            P("seq", "chan"),
            P(None, None, "chan"),
            P(None, None, "chan"),
            P(None, "chan"),
            P("seq", "chan"),
        ),
        out_specs=(P("seq", "chan"), P("seq", None, "chan"), P("seq", "chan")),
        check_vma=False,
    )
```

```python
import math

import jax
import jax.numpy as jnp
from jax import lax
from jax.sharding import PartitionSpec as P


def passed_along(block, axis, distance):
    devices = range(lax.axis_size(axis))
    route = [(i - distance, i) for i in devices if i - distance in devices]
    return lax.ppermute(block, axis, route)


def dft_tables(row_count):
    length = 2 * row_count
    sample = jnp.arange(length, dtype=jnp.int32)
    frequency = jnp.arange(row_count, dtype=jnp.int32)
    angles = (frequency[:, None] * sample[None, :] % length).astype(jnp.float32) * (
        2.0 * math.pi / length
    )
    parity = 1.0 - 2.0 * (sample % 2).astype(jnp.float32)
    lower_rows = jnp.where(frequency[:, None] == 0, parity[None, :], -jnp.sin(angles))
    forward = jnp.concatenate([jnp.cos(angles), lower_rows], axis=0)
    out_index = row_count + frequency
    back_angles = (out_index[:, None] * frequency[None, :] % length).astype(jnp.float32) * (
        2.0 * math.pi / length
    )
    factor = jnp.where(frequency == 0, 1.0, 2.0) / length
    out_parity = 1.0 - 2.0 * (out_index % 2).astype(jnp.float32)
    real_part = jnp.cos(back_angles) * factor[None, :]
    imag_part = jnp.where(
        frequency[None, :] == 0, out_parity[:, None] / length, -2.0 * jnp.sin(back_angles) / length
    )
    inverse = jnp.concatenate([real_part, imag_part], axis=1)
    return (forward, inverse)


def spectral_product(left_spec, right_spec):
    half_len = left_spec.shape[-1] // 2
    left_spec = left_spec.astype(jnp.float32)
    right_spec = right_spec.astype(jnp.float32)
    left_re, left_im = (left_spec[..., :half_len], left_spec[..., half_len:])
    right_re, right_im = (right_spec[..., :half_len], right_spec[..., half_len:])
    first_row = lax.broadcasted_iota(jnp.int32, (1,) * (left_spec.ndim - 1) + (half_len,), left_spec.ndim - 1) == 0
    cross_term = left_im * right_im
    real_out = left_re * right_re - jnp.where(first_row, 0.0, cross_term)
    imag_out = jnp.where(first_row, cross_term, left_re * right_im + left_im * right_re)
    return jnp.concatenate([real_out, imag_out], axis=-1)


def spectral_adjoint(left_spec, grad_spec):
    half_len = left_spec.shape[-1] // 2
    left_spec = left_spec.astype(jnp.float32)
    grad_spec = grad_spec.astype(jnp.float32)
    left_re, left_im = (left_spec[..., :half_len], left_spec[..., half_len:])
    grad_re, grad_im = (grad_spec[..., :half_len], grad_spec[..., half_len:])
    first_row = lax.broadcasted_iota(jnp.int32, (1,) * (left_spec.ndim - 1) + (half_len,), left_spec.ndim - 1) == 0
    cross_term = left_im * grad_im
    real_out = left_re * grad_re + jnp.where(first_row, 0.0, cross_term)
    imag_out = jnp.where(first_row, cross_term, left_re * grad_im - left_im * grad_re)
    return jnp.concatenate([real_out, imag_out], axis=-1)


def neighbour_rows(edge_rows, offset):
    return passed_along(edge_rows, "seq", offset)


def swap_layout(values):
    return lax.all_to_all(values, "seq", 1, 1, tiled=True)


def on_device(tokens, in_weight, short_weight, filter_taps, cotangent):
    row_count, local_width = tokens.shape
    seq_count = lax.axis_size("seq")
    chan_count = lax.axis_size("chan")
    group = local_width // seq_count
    own_block = lax.axis_index("seq")
    forward, inverse = dft_tables(row_count)
    full_table = forward.astype(jnp.bfloat16)
    half_table = full_table[:, :row_count]
    back_table = inverse.astype(jnp.bfloat16)

    half_count = chan_count // 2
    core = lax.axis_index("chan") % 2
    groups = [[2 * j + k for j in range(half_count)] for k in range(2)]
    copies = jnp.broadcast_to(tokens[None], (half_count,) + tokens.shape)
    same_core = lax.all_to_all(copies, "chan", 0, 0, tiled=True, axis_index_groups=groups)
    other_core = lax.ppermute(same_core, "chan", [(i, i ^ 1) for i in range(chan_count)])
    weight_pairs = in_weight.reshape(half_count, 2, local_width, 3, local_width)
    own_weights = lax.dynamic_index_in_dim(weight_pairs, core, axis=1, keepdims=False)
    other_weights = lax.dynamic_index_in_dim(weight_pairs, 1 - core, axis=1, keepdims=False)
    streams = (
        jnp.einsum("stf,sfqc->qtc", same_core, own_weights, preferred_element_type=jnp.float32)
        + jnp.einsum(
            "stf,sfqc->qtc", other_core, other_weights, preferred_element_type=jnp.float32
        )
    ).astype(jnp.bfloat16)
    before = neighbour_rows(streams[:, row_count - 2 :], 1)
    extended = jnp.concatenate([before, streams], axis=1).astype(jnp.float32)
    conv_weight = short_weight[:, :, None, :]
    conv_out = (
        conv_weight[:, 0] * extended[:, 2:]
        + conv_weight[:, 1] * extended[:, 1:-1]
        + conv_weight[:, 2] * extended[:, :-2]
    )
    query_conv, key_conv, value_conv = (conv_out[0], conv_out[1], conv_out[2])
    gated = (key_conv * value_conv).astype(jnp.bfloat16)
    grad_long = (cotangent.astype(jnp.float32) * query_conv).astype(jnp.bfloat16)

    both_cols = swap_layout(
        jnp.concatenate(
            [gated.reshape(row_count, seq_count, group), grad_long.reshape(row_count, seq_count, group)],
            axis=2,
        )
    )
    gated_cols, grad_long_cols = (both_cols[..., :group], both_cols[..., group:])

    after_rows, _ = lax.optimization_barrier(
        (jnp.concatenate([streams[:, :2], cotangent[None, :2]], axis=0), both_cols)
    )
    after = neighbour_rows(after_rows, -1)
    next_streams, next_cot = (after[:3], after[3])
    edge = jnp.concatenate([streams[:, row_count - 2 :], next_streams], axis=1).astype(jnp.float32)
    edge_out = (
        conv_weight[:, 0] * edge[:, 2:]
        + conv_weight[:, 1] * edge[:, 1:-1]
        + conv_weight[:, 2] * edge[:, :-2]
    )
    query_conv = jnp.concatenate([query_conv, edge_out[0]], axis=0)
    key_conv = jnp.concatenate([key_conv, edge_out[1]], axis=0)
    value_conv = jnp.concatenate([value_conv, edge_out[2]], axis=0)
    cot_wide = jnp.concatenate([cotangent, next_cot], axis=0).astype(jnp.float32)
    own_spec = jnp.einsum(
        "tbc,kt->bck", gated_cols, half_table, preferred_element_type=jnp.float32
    ).astype(jnp.bfloat16)
    own_taps = lax.dynamic_slice_in_dim(filter_taps, own_block * group, group, axis=1)
    tap_blocks = own_taps.reshape(seq_count, row_count, group)
    earlier = jnp.concatenate(
        [jnp.zeros((1, row_count, group), jnp.bfloat16), tap_blocks[:-1]], axis=0
    )
    segments = jnp.concatenate([earlier, tap_blocks], axis=1)
    filters = jnp.einsum(
        "fn,bnc->bcf", full_table, segments, preferred_element_type=jnp.float32
    ).astype(jnp.bfloat16)

    mixed_spec = jnp.zeros(own_spec.shape, jnp.float32)
    for lag_step in range(seq_count):
        term = spectral_product(filters[lag_step][None], own_spec[: seq_count - lag_step])
        mixed_spec = mixed_spec + jnp.pad(term, ((lag_step, 0), (0, 0), (0, 0)))
    long_cols = jnp.einsum(
        "bck,ak->abc", mixed_spec.astype(jnp.bfloat16), back_table,
        preferred_element_type=jnp.float32,
    ).astype(jnp.bfloat16)

    grad_spec = jnp.einsum(
        "abc,ak->bck", grad_long_cols, back_table, preferred_element_type=jnp.float32
    ).astype(jnp.bfloat16)
    spectral_grad = jnp.zeros(grad_spec.shape, jnp.float32)
    filter_parts = []
    for lag_step in range(seq_count):
        ahead = grad_spec[lag_step:]
        term = spectral_adjoint(filters[lag_step][None], ahead)
        spectral_grad = spectral_grad + jnp.pad(term, ((0, lag_step), (0, 0), (0, 0)))
        filter_parts.append(
            jnp.sum(spectral_adjoint(own_spec[: seq_count - lag_step], ahead), axis=0)
        )
    filter_grad = jnp.stack(filter_parts, axis=0)
    gated_grad_cols = jnp.einsum(
        "bck,kt->tbc", spectral_grad.astype(jnp.bfloat16), half_table,
        preferred_element_type=jnp.float32,
    ).astype(jnp.bfloat16)

    tap_spec = jnp.einsum("dck,kn->dcn", filter_grad, forward, precision=lax.Precision.HIGHEST)
    tap_cols = tap_spec[:, :, row_count:] + jnp.concatenate(
        [tap_spec[1:, :, :row_count], jnp.zeros((1, group, row_count), jnp.float32)], axis=0
    )
    tap_cols = tap_cols.transpose(2, 0, 1).astype(jnp.bfloat16)

    def with_next_rows(cols):
        following = jnp.concatenate(
            [cols[:2, 1:], jnp.zeros((2, 1, group), cols.dtype)], axis=1
        )
        return jnp.concatenate([cols, following], axis=0)

    returned = swap_layout(
        jnp.concatenate(
            [
                with_next_rows(long_cols),
                with_next_rows(gated_grad_cols),
                jnp.concatenate([tap_cols, jnp.zeros((2, seq_count, group), jnp.bfloat16)], axis=0),
            ],
            axis=2,
        )
    )
    wide_rows = row_count + 2
    long_out = returned[..., :group].reshape(wide_rows, local_width).astype(jnp.float32)
    gated_wide = returned[..., group : 2 * group].reshape(wide_rows, local_width).astype(jnp.float32)
    tap_grads = returned[:row_count, :, 2 * group :].astype(jnp.float32).reshape(row_count, local_width)

    operator_out = (query_conv[:row_count] * long_out[:row_count]).astype(jnp.bfloat16)
    grad_query = cot_wide * long_out
    grad_streams = jnp.stack(
        [grad_query, gated_wide * value_conv, gated_wide * key_conv], axis=0
    ).astype(jnp.bfloat16).astype(jnp.float32)
    stream_grads = (
        conv_weight[:, 0] * grad_streams[:, :row_count]
        + conv_weight[:, 1] * grad_streams[:, 1 : row_count + 1]
        + conv_weight[:, 2] * grad_streams[:, 2:]
    ).astype(jnp.bfloat16).transpose(1, 0, 2)
    return (operator_out, stream_grads, tap_grads)


def solution(mesh):
    return jax.shard_map(
        on_device,
        mesh=mesh,
        in_specs=(
            P("seq", "chan"),
            P(None, None, "chan"),
            P(None, None, "chan"),
            P(None, "chan"),
            P("seq", "chan"),
        ),
        out_specs=(P("seq", "chan"), P("seq", None, "chan"), P("seq", "chan")),
        check_vma=False,
    )
```

```python
import math

import jax
import jax.numpy as jnp
from jax import lax
from jax.sharding import PartitionSpec as P


def passed_along(block, axis, distance):
    devices = range(lax.axis_size(axis))
    route = [(i - distance, i) for i in devices if i - distance in devices]
    return lax.ppermute(block, axis, route)


def dft_tables(row_count):
    length = 2 * row_count
    sample = jnp.arange(length, dtype=jnp.int32)
    frequency = jnp.arange(row_count, dtype=jnp.int32)
    base = sample.astype(jnp.float32) * (2.0 * math.pi / length)
    cos_base, sin_base = (jnp.cos(base), jnp.sin(base))
    phase = frequency[:, None] * sample[None, :] % length
    parity = 1.0 - 2.0 * (sample % 2).astype(jnp.float32)
    lower_rows = jnp.where(frequency[:, None] == 0, parity[None, :], -jnp.take(sin_base, phase))
    forward = jnp.concatenate([jnp.take(cos_base, phase), lower_rows], axis=0)
    out_index = row_count + frequency
    back_phase = out_index[:, None] * frequency[None, :] % length
    factor = jnp.where(frequency == 0, 1.0, 2.0) / length
    out_parity = 1.0 - 2.0 * (out_index % 2).astype(jnp.float32)
    real_part = jnp.take(cos_base, back_phase) * factor[None, :]
    imag_part = jnp.where(
        frequency[None, :] == 0,
        out_parity[:, None] / length,
        -2.0 * jnp.take(sin_base, back_phase) / length,
    )
    inverse = jnp.concatenate([real_part, imag_part], axis=1)
    return (forward, inverse)


def spectral_product(left_spec, right_spec):
    half_len = left_spec.shape[-1] // 2
    left_spec = left_spec.astype(jnp.float32)
    right_spec = right_spec.astype(jnp.float32)
    left_re, left_im = (left_spec[..., :half_len], left_spec[..., half_len:])
    right_re, right_im = (right_spec[..., :half_len], right_spec[..., half_len:])
    first_row = lax.broadcasted_iota(jnp.int32, (1,) * (left_spec.ndim - 1) + (half_len,), left_spec.ndim - 1) == 0
    cross_term = left_im * right_im
    real_out = left_re * right_re - jnp.where(first_row, 0.0, cross_term)
    imag_out = jnp.where(first_row, cross_term, left_re * right_im + left_im * right_re)
    return jnp.concatenate([real_out, imag_out], axis=-1)


def spectral_adjoint(left_spec, grad_spec):
    half_len = left_spec.shape[-1] // 2
    left_spec = left_spec.astype(jnp.float32)
    grad_spec = grad_spec.astype(jnp.float32)
    left_re, left_im = (left_spec[..., :half_len], left_spec[..., half_len:])
    grad_re, grad_im = (grad_spec[..., :half_len], grad_spec[..., half_len:])
    first_row = lax.broadcasted_iota(jnp.int32, (1,) * (left_spec.ndim - 1) + (half_len,), left_spec.ndim - 1) == 0
    cross_term = left_im * grad_im
    real_out = left_re * grad_re + jnp.where(first_row, 0.0, cross_term)
    imag_out = jnp.where(first_row, cross_term, left_re * grad_im - left_im * grad_re)
    return jnp.concatenate([real_out, imag_out], axis=-1)


def neighbour_rows(edge_rows, offset):
    return passed_along(edge_rows, "seq", offset)


def swap_layout(values):
    return lax.all_to_all(values, "seq", 1, 1, tiled=True)


def on_device(tokens, in_weight, short_weight, filter_taps, cotangent):
    row_count, local_width = tokens.shape
    seq_count = lax.axis_size("seq")
    chan_count = lax.axis_size("chan")
    group = local_width // seq_count
    own_block = lax.axis_index("seq")
    forward, inverse = dft_tables(row_count)
    full_table = forward.astype(jnp.bfloat16)
    half_table = full_table[:, :row_count]
    back_table = inverse.astype(jnp.bfloat16)

    half_count = chan_count // 2
    core = lax.axis_index("chan") % 2
    groups = [[2 * j + k for j in range(half_count)] for k in range(2)]
    copies = jnp.broadcast_to(tokens[None], (half_count,) + tokens.shape)
    same_core = lax.all_to_all(copies, "chan", 0, 0, tiled=True, axis_index_groups=groups)
    other_core = lax.ppermute(same_core, "chan", [(i, i ^ 1) for i in range(chan_count)])
    weight_pairs = in_weight.reshape(half_count, 2, local_width, 3, local_width)
    own_weights = lax.dynamic_index_in_dim(weight_pairs, core, axis=1, keepdims=False)
    other_weights = lax.dynamic_index_in_dim(weight_pairs, 1 - core, axis=1, keepdims=False)
    streams = (
        jnp.einsum("stf,sfqc->qtc", same_core, own_weights, preferred_element_type=jnp.float32)
        + jnp.einsum(
            "stf,sfqc->qtc", other_core, other_weights, preferred_element_type=jnp.float32
        )
    ).astype(jnp.bfloat16)
    before = neighbour_rows(streams[:, row_count - 2 :], 1)
    extended = jnp.concatenate([before, streams], axis=1).astype(jnp.float32)
    conv_weight = short_weight[:, :, None, :]
    conv_out = (
        conv_weight[:, 0] * extended[:, 2:]
        + conv_weight[:, 1] * extended[:, 1:-1]
        + conv_weight[:, 2] * extended[:, :-2]
    )
    query_conv, key_conv, value_conv = (conv_out[0], conv_out[1], conv_out[2])
    gated = (key_conv * value_conv).astype(jnp.bfloat16)
    grad_long = (cotangent.astype(jnp.float32) * query_conv).astype(jnp.bfloat16)

    both_cols = swap_layout(
        jnp.concatenate(
            [gated.reshape(row_count, seq_count, group), grad_long.reshape(row_count, seq_count, group)],
            axis=2,
        )
    )
    gated_cols, grad_long_cols = (both_cols[..., :group], both_cols[..., group:])

    after_rows, _ = lax.optimization_barrier(
        (jnp.concatenate([streams[:, :2], cotangent[None, :2]], axis=0), both_cols)
    )
    after = neighbour_rows(after_rows, -1)
    next_streams, next_cot = (after[:3], after[3])
    edge = jnp.concatenate([streams[:, row_count - 2 :], next_streams], axis=1).astype(jnp.float32)
    edge_out = (
        conv_weight[:, 0] * edge[:, 2:]
        + conv_weight[:, 1] * edge[:, 1:-1]
        + conv_weight[:, 2] * edge[:, :-2]
    )
    query_conv = jnp.concatenate([query_conv, edge_out[0]], axis=0)
    key_conv = jnp.concatenate([key_conv, edge_out[1]], axis=0)
    value_conv = jnp.concatenate([value_conv, edge_out[2]], axis=0)
    cot_wide = jnp.concatenate([cotangent, next_cot], axis=0).astype(jnp.float32)
    own_spec = jnp.einsum(
        "tbc,kt->bck", gated_cols, half_table, preferred_element_type=jnp.float32
    ).astype(jnp.bfloat16)
    own_taps = lax.dynamic_slice_in_dim(filter_taps, own_block * group, group, axis=1)
    tap_blocks = own_taps.reshape(seq_count, row_count, group)
    earlier = jnp.concatenate(
        [jnp.zeros((1, row_count, group), jnp.bfloat16), tap_blocks[:-1]], axis=0
    )
    segments = jnp.concatenate([earlier, tap_blocks], axis=1)
    filters = jnp.einsum(
        "fn,bnc->bcf", full_table, segments, preferred_element_type=jnp.float32
    ).astype(jnp.bfloat16)

    mixed_spec = jnp.zeros(own_spec.shape, jnp.float32)
    for lag_step in range(seq_count):
        term = spectral_product(filters[lag_step][None], own_spec[: seq_count - lag_step])
        mixed_spec = mixed_spec + jnp.pad(term, ((lag_step, 0), (0, 0), (0, 0)))
    long_cols = jnp.einsum(
        "bck,ak->abc", mixed_spec.astype(jnp.bfloat16), back_table,
        preferred_element_type=jnp.float32,
    ).astype(jnp.bfloat16)

    grad_spec = jnp.einsum(
        "abc,ak->bck", grad_long_cols, back_table, preferred_element_type=jnp.float32
    ).astype(jnp.bfloat16)
    spectral_grad = jnp.zeros(grad_spec.shape, jnp.float32)
    filter_parts = []
    for lag_step in range(seq_count):
        ahead = grad_spec[lag_step:]
        term = spectral_adjoint(filters[lag_step][None], ahead)
        spectral_grad = spectral_grad + jnp.pad(term, ((0, lag_step), (0, 0), (0, 0)))
        filter_parts.append(
            jnp.sum(spectral_adjoint(own_spec[: seq_count - lag_step], ahead), axis=0)
        )
    filter_grad = jnp.stack(filter_parts, axis=0)
    gated_grad_cols = jnp.einsum(
        "bck,kt->tbc", spectral_grad.astype(jnp.bfloat16), half_table,
        preferred_element_type=jnp.float32,
    ).astype(jnp.bfloat16)

    tap_spec = jnp.einsum("dck,kn->dcn", filter_grad, forward, precision=lax.Precision.HIGHEST)
    tap_cols = tap_spec[:, :, row_count:] + jnp.concatenate(
        [tap_spec[1:, :, :row_count], jnp.zeros((1, group, row_count), jnp.float32)], axis=0
    )
    tap_cols = tap_cols.transpose(2, 0, 1).astype(jnp.bfloat16)

    def with_next_rows(cols):
        following = jnp.concatenate(
            [cols[:2, 1:], jnp.zeros((2, 1, group), cols.dtype)], axis=1
        )
        return jnp.concatenate([cols, following], axis=0)

    returned = swap_layout(
        jnp.concatenate(
            [
                with_next_rows(long_cols),
                with_next_rows(gated_grad_cols),
                jnp.concatenate([tap_cols, jnp.zeros((2, seq_count, group), jnp.bfloat16)], axis=0),
            ],
            axis=2,
        )
    )
    wide_rows = row_count + 2
    long_out = returned[..., :group].reshape(wide_rows, local_width).astype(jnp.float32)
    gated_wide = returned[..., group : 2 * group].reshape(wide_rows, local_width).astype(jnp.float32)
    tap_grads = returned[:row_count, :, 2 * group :].astype(jnp.float32).reshape(row_count, local_width)

    operator_out = (query_conv[:row_count] * long_out[:row_count]).astype(jnp.bfloat16)
    grad_query = cot_wide * long_out
    grad_streams = jnp.stack(
        [grad_query, gated_wide * value_conv, gated_wide * key_conv], axis=0
    ).astype(jnp.bfloat16).astype(jnp.float32)
    stream_grads = (
        conv_weight[:, 0] * grad_streams[:, :row_count]
        + conv_weight[:, 1] * grad_streams[:, 1 : row_count + 1]
        + conv_weight[:, 2] * grad_streams[:, 2:]
    ).astype(jnp.bfloat16).transpose(1, 0, 2)
    return (operator_out, stream_grads, tap_grads)


def solution(mesh):
    return jax.shard_map(
        on_device,
        mesh=mesh,
        in_specs=(
            P("seq", "chan"),
            P(None, None, "chan"),
            P(None, None, "chan"),
            P(None, "chan"),
            P("seq", "chan"),
        ),
        out_specs=(P("seq", "chan"), P("seq", None, "chan"), P("seq", "chan")),
        check_vma=False,
    )
```

```python
import math

import jax
import jax.numpy as jnp
from jax import lax
from jax.sharding import PartitionSpec as P


def passed_along(block, axis, distance):
    devices = range(lax.axis_size(axis))
    route = [(i - distance, i) for i in devices if i - distance in devices]
    return lax.ppermute(block, axis, route)


def dft_tables(row_count, sample, frequency):
    length = 2 * row_count
    angles = (frequency[:, None] * sample[None, :] % length).astype(jnp.float32) * (
        2.0 * math.pi / length
    )
    parity = 1.0 - 2.0 * (sample % 2).astype(jnp.float32)
    lower_rows = jnp.where(frequency[:, None] == 0, parity[None, :], -jnp.sin(angles))
    forward = jnp.concatenate([jnp.cos(angles), lower_rows], axis=0)
    out_index = row_count + frequency
    back_angles = (out_index[:, None] * frequency[None, :] % length).astype(jnp.float32) * (
        2.0 * math.pi / length
    )
    factor = jnp.where(frequency == 0, 1.0, 2.0) / length
    out_parity = 1.0 - 2.0 * (out_index % 2).astype(jnp.float32)
    real_part = jnp.cos(back_angles) * factor[None, :]
    imag_part = jnp.where(
        frequency[None, :] == 0, out_parity[:, None] / length, -2.0 * jnp.sin(back_angles) / length
    )
    inverse = jnp.concatenate([real_part, imag_part], axis=1)
    return (forward, inverse)


def spectral_product(left_spec, right_spec):
    half_len = left_spec.shape[-1] // 2
    left_spec = left_spec.astype(jnp.float32)
    right_spec = right_spec.astype(jnp.float32)
    left_re, left_im = (left_spec[..., :half_len], left_spec[..., half_len:])
    right_re, right_im = (right_spec[..., :half_len], right_spec[..., half_len:])
    first_row = lax.broadcasted_iota(jnp.int32, (1,) * (left_spec.ndim - 1) + (half_len,), left_spec.ndim - 1) == 0
    cross_term = left_im * right_im
    real_out = left_re * right_re - jnp.where(first_row, 0.0, cross_term)
    imag_out = jnp.where(first_row, cross_term, left_re * right_im + left_im * right_re)
    return jnp.concatenate([real_out, imag_out], axis=-1)


def spectral_adjoint(left_spec, grad_spec):
    half_len = left_spec.shape[-1] // 2
    left_spec = left_spec.astype(jnp.float32)
    grad_spec = grad_spec.astype(jnp.float32)
    left_re, left_im = (left_spec[..., :half_len], left_spec[..., half_len:])
    grad_re, grad_im = (grad_spec[..., :half_len], grad_spec[..., half_len:])
    first_row = lax.broadcasted_iota(jnp.int32, (1,) * (left_spec.ndim - 1) + (half_len,), left_spec.ndim - 1) == 0
    cross_term = left_im * grad_im
    real_out = left_re * grad_re + jnp.where(first_row, 0.0, cross_term)
    imag_out = jnp.where(first_row, cross_term, left_re * grad_im - left_im * grad_re)
    return jnp.concatenate([real_out, imag_out], axis=-1)


def neighbour_rows(edge_rows, offset):
    return passed_along(edge_rows, "seq", offset)


def swap_layout(values):
    return lax.all_to_all(values, "seq", 1, 1, tiled=True)


def on_device(tokens, in_weight, short_weight, filter_taps, cotangent):
    row_count, local_width = tokens.shape
    seq_count = lax.axis_size("seq")
    chan_count = lax.axis_size("chan")
    group = local_width // seq_count
    own_block = lax.axis_index("seq")
    forward = dft_tables(
        row_count, jnp.arange(2 * row_count, dtype=jnp.int32), jnp.arange(row_count, dtype=jnp.int32)
    )[0]
    full_table = forward.astype(jnp.bfloat16)
    half_table = full_table[:, :row_count]

    half_count = chan_count // 2
    core = lax.axis_index("chan") % 2
    groups = [[2 * j + k for j in range(half_count)] for k in range(2)]
    copies = jnp.broadcast_to(tokens[None], (half_count,) + tokens.shape)
    same_core = lax.all_to_all(copies, "chan", 0, 0, tiled=True, axis_index_groups=groups)
    other_core = lax.ppermute(same_core, "chan", [(i, i ^ 1) for i in range(chan_count)])
    weight_pairs = in_weight.reshape(half_count, 2, local_width, 3, local_width)
    own_weights = lax.dynamic_index_in_dim(weight_pairs, core, axis=1, keepdims=False)
    other_weights = lax.dynamic_index_in_dim(weight_pairs, 1 - core, axis=1, keepdims=False)
    streams = (
        jnp.einsum("stf,sfqc->qtc", same_core, own_weights, preferred_element_type=jnp.float32)
        + jnp.einsum(
            "stf,sfqc->qtc", other_core, other_weights, preferred_element_type=jnp.float32
        )
    ).astype(jnp.bfloat16)
    before = neighbour_rows(streams[:, row_count - 2 :], 1)
    extended = jnp.concatenate([before, streams], axis=1).astype(jnp.float32)
    conv_weight = short_weight[:, :, None, :]
    conv_out = (
        conv_weight[:, 0] * extended[:, 2:]
        + conv_weight[:, 1] * extended[:, 1:-1]
        + conv_weight[:, 2] * extended[:, :-2]
    )
    query_conv, key_conv, value_conv = (conv_out[0], conv_out[1], conv_out[2])
    gated = (key_conv * value_conv).astype(jnp.bfloat16)
    grad_long = (cotangent.astype(jnp.float32) * query_conv).astype(jnp.bfloat16)

    inbound = jnp.concatenate(
        [gated.reshape(row_count, seq_count, group), grad_long.reshape(row_count, seq_count, group)],
        axis=2,
    )
    both_cols = swap_layout(inbound)
    indices, _ = lax.optimization_barrier(
        (
            (jnp.arange(2 * row_count, dtype=jnp.int32), jnp.arange(row_count, dtype=jnp.int32)),
            inbound,
        )
    )
    inverse = dft_tables(row_count, *indices)[1]
    back_table = inverse.astype(jnp.bfloat16)
    gated_cols, grad_long_cols = (both_cols[..., :group], both_cols[..., group:])

    after_rows, _ = lax.optimization_barrier(
        (jnp.concatenate([streams[:, :2], cotangent[None, :2]], axis=0), both_cols)
    )
    after = neighbour_rows(after_rows, -1)
    next_streams, next_cot = (after[:3], after[3])
    edge = jnp.concatenate([streams[:, row_count - 2 :], next_streams], axis=1).astype(jnp.float32)
    edge_out = (
        conv_weight[:, 0] * edge[:, 2:]
        + conv_weight[:, 1] * edge[:, 1:-1]
        + conv_weight[:, 2] * edge[:, :-2]
    )
    query_conv = jnp.concatenate([query_conv, edge_out[0]], axis=0)
    key_conv = jnp.concatenate([key_conv, edge_out[1]], axis=0)
    value_conv = jnp.concatenate([value_conv, edge_out[2]], axis=0)
    cot_wide = jnp.concatenate([cotangent, next_cot], axis=0).astype(jnp.float32)
    own_spec = jnp.einsum(
        "tbc,kt->bck", gated_cols, half_table, preferred_element_type=jnp.float32
    ).astype(jnp.bfloat16)
    own_taps = lax.dynamic_slice_in_dim(filter_taps, own_block * group, group, axis=1)
    tap_blocks = own_taps.reshape(seq_count, row_count, group)
    earlier = jnp.concatenate(
        [jnp.zeros((1, row_count, group), jnp.bfloat16), tap_blocks[:-1]], axis=0
    )
    segments = jnp.concatenate([earlier, tap_blocks], axis=1)
    filters = jnp.einsum(
        "fn,bnc->bcf", full_table, segments, preferred_element_type=jnp.float32
    ).astype(jnp.bfloat16)

    mixed_spec = jnp.zeros(own_spec.shape, jnp.float32)
    for lag_step in range(seq_count):
        term = spectral_product(filters[lag_step][None], own_spec[: seq_count - lag_step])
        mixed_spec = mixed_spec + jnp.pad(term, ((lag_step, 0), (0, 0), (0, 0)))
    long_cols = jnp.einsum(
        "bck,ak->abc", mixed_spec.astype(jnp.bfloat16), back_table,
        preferred_element_type=jnp.float32,
    ).astype(jnp.bfloat16)

    grad_spec = jnp.einsum(
        "abc,ak->bck", grad_long_cols, back_table, preferred_element_type=jnp.float32
    ).astype(jnp.bfloat16)
    spectral_grad = jnp.zeros(grad_spec.shape, jnp.float32)
    filter_parts = []
    for lag_step in range(seq_count):
        ahead = grad_spec[lag_step:]
        term = spectral_adjoint(filters[lag_step][None], ahead)
        spectral_grad = spectral_grad + jnp.pad(term, ((0, lag_step), (0, 0), (0, 0)))
        filter_parts.append(
            jnp.sum(spectral_adjoint(own_spec[: seq_count - lag_step], ahead), axis=0)
        )
    filter_grad = jnp.stack(filter_parts, axis=0)
    gated_grad_cols = jnp.einsum(
        "bck,kt->tbc", spectral_grad.astype(jnp.bfloat16), half_table,
        preferred_element_type=jnp.float32,
    ).astype(jnp.bfloat16)

    tap_spec = jnp.einsum("dck,kn->dcn", filter_grad, forward, precision=lax.Precision.HIGHEST)
    tap_cols = tap_spec[:, :, row_count:] + jnp.concatenate(
        [tap_spec[1:, :, :row_count], jnp.zeros((1, group, row_count), jnp.float32)], axis=0
    )
    tap_cols = tap_cols.transpose(2, 0, 1).astype(jnp.bfloat16)

    def with_next_rows(cols):
        following = jnp.concatenate(
            [cols[:2, 1:], jnp.zeros((2, 1, group), cols.dtype)], axis=1
        )
        return jnp.concatenate([cols, following], axis=0)

    returned = swap_layout(
        jnp.concatenate(
            [
                with_next_rows(long_cols),
                with_next_rows(gated_grad_cols),
                jnp.concatenate([tap_cols, jnp.zeros((2, seq_count, group), jnp.bfloat16)], axis=0),
            ],
            axis=2,
        )
    )
    wide_rows = row_count + 2
    long_out = returned[..., :group].reshape(wide_rows, local_width).astype(jnp.float32)
    gated_wide = returned[..., group : 2 * group].reshape(wide_rows, local_width).astype(jnp.float32)
    tap_grads = returned[:row_count, :, 2 * group :].astype(jnp.float32).reshape(row_count, local_width)

    operator_out = (query_conv[:row_count] * long_out[:row_count]).astype(jnp.bfloat16)
    grad_query = cot_wide * long_out
    grad_streams = jnp.stack(
        [grad_query, gated_wide * value_conv, gated_wide * key_conv], axis=0
    ).astype(jnp.bfloat16).astype(jnp.float32)
    stream_grads = (
        conv_weight[:, 0] * grad_streams[:, :row_count]
        + conv_weight[:, 1] * grad_streams[:, 1 : row_count + 1]
        + conv_weight[:, 2] * grad_streams[:, 2:]
    ).astype(jnp.bfloat16).transpose(1, 0, 2)
    return (operator_out, stream_grads, tap_grads)


def solution(mesh):
    return jax.shard_map(
        on_device,
        mesh=mesh,
        in_specs=(
            P("seq", "chan"),
            P(None, None, "chan"),
            P(None, None, "chan"),
            P(None, "chan"),
            P("seq", "chan"),
        ),
        out_specs=(P("seq", "chan"), P("seq", None, "chan"), P("seq", "chan")),
        check_vma=False,
    )
```

```python
import math

import jax
import jax.numpy as jnp
from jax import lax
from jax.sharding import PartitionSpec as P


def passed_along(block, axis, distance):
    devices = range(lax.axis_size(axis))
    route = [(i - distance, i) for i in devices if i - distance in devices]
    return lax.ppermute(block, axis, route)


def dft_tables(row_count):
    length = 2 * row_count
    sample = jnp.arange(length, dtype=jnp.int32)
    frequency = jnp.arange(row_count, dtype=jnp.int32)
    first_half = sample[:row_count]
    angles = (frequency[:, None] * first_half[None, :] % length).astype(jnp.float32) * (
        2.0 * math.pi / length
    )
    parity = 1.0 - 2.0 * (first_half % 2).astype(jnp.float32)
    lower_rows = jnp.where(frequency[:, None] == 0, parity[None, :], -jnp.sin(angles))
    left = jnp.concatenate([jnp.cos(angles), lower_rows], axis=0)
    row_sign = 1.0 - 2.0 * (frequency % 2).astype(jnp.float32)
    row_sign = jnp.concatenate([row_sign, row_sign])[:, None]
    forward = jnp.concatenate([left, left * row_sign], axis=1)
    out_index = row_count + frequency
    back_angles = (out_index[:, None] * frequency[None, :] % length).astype(jnp.float32) * (
        2.0 * math.pi / length
    )
    factor = jnp.where(frequency == 0, 1.0, 2.0) / length
    out_parity = 1.0 - 2.0 * (out_index % 2).astype(jnp.float32)
    real_part = jnp.cos(back_angles) * factor[None, :]
    imag_part = jnp.where(
        frequency[None, :] == 0, out_parity[:, None] / length, -2.0 * jnp.sin(back_angles) / length
    )
    inverse = jnp.concatenate([real_part, imag_part], axis=1)
    return (forward, inverse)


def spectral_product(left_spec, right_spec):
    half_len = left_spec.shape[-1] // 2
    left_spec = left_spec.astype(jnp.float32)
    right_spec = right_spec.astype(jnp.float32)
    left_re, left_im = (left_spec[..., :half_len], left_spec[..., half_len:])
    right_re, right_im = (right_spec[..., :half_len], right_spec[..., half_len:])
    first_row = lax.broadcasted_iota(jnp.int32, (1,) * (left_spec.ndim - 1) + (half_len,), left_spec.ndim - 1) == 0
    cross_term = left_im * right_im
    real_out = left_re * right_re - jnp.where(first_row, 0.0, cross_term)
    imag_out = jnp.where(first_row, cross_term, left_re * right_im + left_im * right_re)
    return jnp.concatenate([real_out, imag_out], axis=-1)


def spectral_adjoint(left_spec, grad_spec):
    half_len = left_spec.shape[-1] // 2
    left_spec = left_spec.astype(jnp.float32)
    grad_spec = grad_spec.astype(jnp.float32)
    left_re, left_im = (left_spec[..., :half_len], left_spec[..., half_len:])
    grad_re, grad_im = (grad_spec[..., :half_len], grad_spec[..., half_len:])
    first_row = lax.broadcasted_iota(jnp.int32, (1,) * (left_spec.ndim - 1) + (half_len,), left_spec.ndim - 1) == 0
    cross_term = left_im * grad_im
    real_out = left_re * grad_re + jnp.where(first_row, 0.0, cross_term)
    imag_out = jnp.where(first_row, cross_term, left_re * grad_im - left_im * grad_re)
    return jnp.concatenate([real_out, imag_out], axis=-1)


def neighbour_rows(edge_rows, offset):
    return passed_along(edge_rows, "seq", offset)


def swap_layout(values):
    return lax.all_to_all(values, "seq", 1, 1, tiled=True)


def on_device(tokens, in_weight, short_weight, filter_taps, cotangent):
    row_count, local_width = tokens.shape
    seq_count = lax.axis_size("seq")
    chan_count = lax.axis_size("chan")
    group = local_width // seq_count
    own_block = lax.axis_index("seq")
    forward, inverse = dft_tables(row_count)
    full_table = forward.astype(jnp.bfloat16)
    half_table = full_table[:, :row_count]
    back_table = inverse.astype(jnp.bfloat16)

    half_count = chan_count // 2
    core = lax.axis_index("chan") % 2
    groups = [[2 * j + k for j in range(half_count)] for k in range(2)]
    copies = jnp.broadcast_to(tokens[None], (half_count,) + tokens.shape)
    same_core = lax.all_to_all(copies, "chan", 0, 0, tiled=True, axis_index_groups=groups)
    other_core = lax.ppermute(same_core, "chan", [(i, i ^ 1) for i in range(chan_count)])
    weight_pairs = in_weight.reshape(half_count, 2, local_width, 3, local_width)
    own_weights = lax.dynamic_index_in_dim(weight_pairs, core, axis=1, keepdims=False)
    other_weights = lax.dynamic_index_in_dim(weight_pairs, 1 - core, axis=1, keepdims=False)
    streams = (
        jnp.einsum("stf,sfqc->qtc", same_core, own_weights, preferred_element_type=jnp.float32)
        + jnp.einsum(
            "stf,sfqc->qtc", other_core, other_weights, preferred_element_type=jnp.float32
        )
    ).astype(jnp.bfloat16)
    before = neighbour_rows(streams[:, row_count - 2 :], 1)
    extended = jnp.concatenate([before, streams], axis=1).astype(jnp.float32)
    conv_weight = short_weight[:, :, None, :]
    conv_out = (
        conv_weight[:, 0] * extended[:, 2:]
        + conv_weight[:, 1] * extended[:, 1:-1]
        + conv_weight[:, 2] * extended[:, :-2]
    )
    query_conv, key_conv, value_conv = (conv_out[0], conv_out[1], conv_out[2])
    gated = (key_conv * value_conv).astype(jnp.bfloat16)
    grad_long = (cotangent.astype(jnp.float32) * query_conv).astype(jnp.bfloat16)

    both_cols = swap_layout(
        jnp.concatenate(
            [gated.reshape(row_count, seq_count, group), grad_long.reshape(row_count, seq_count, group)],
            axis=2,
        )
    )
    gated_cols, grad_long_cols = (both_cols[..., :group], both_cols[..., group:])

    after_rows, _ = lax.optimization_barrier(
        (jnp.concatenate([streams[:, :2], cotangent[None, :2]], axis=0), both_cols)
    )
    after = neighbour_rows(after_rows, -1)
    next_streams, next_cot = (after[:3], after[3])
    edge = jnp.concatenate([streams[:, row_count - 2 :], next_streams], axis=1).astype(jnp.float32)
    edge_out = (
        conv_weight[:, 0] * edge[:, 2:]
        + conv_weight[:, 1] * edge[:, 1:-1]
        + conv_weight[:, 2] * edge[:, :-2]
    )
    query_conv = jnp.concatenate([query_conv, edge_out[0]], axis=0)
    key_conv = jnp.concatenate([key_conv, edge_out[1]], axis=0)
    value_conv = jnp.concatenate([value_conv, edge_out[2]], axis=0)
    cot_wide = jnp.concatenate([cotangent, next_cot], axis=0).astype(jnp.float32)
    own_spec = jnp.einsum(
        "tbc,kt->bck", gated_cols, half_table, preferred_element_type=jnp.float32
    ).astype(jnp.bfloat16)
    own_taps = lax.dynamic_slice_in_dim(filter_taps, own_block * group, group, axis=1)
    tap_blocks = own_taps.reshape(seq_count, row_count, group)
    earlier = jnp.concatenate(
        [jnp.zeros((1, row_count, group), jnp.bfloat16), tap_blocks[:-1]], axis=0
    )
    segments = jnp.concatenate([earlier, tap_blocks], axis=1)
    filters = jnp.einsum(
        "fn,bnc->bcf", full_table, segments, preferred_element_type=jnp.float32
    ).astype(jnp.bfloat16)

    mixed_spec = jnp.zeros(own_spec.shape, jnp.float32)
    for lag_step in range(seq_count):
        term = spectral_product(filters[lag_step][None], own_spec[: seq_count - lag_step])
        mixed_spec = mixed_spec + jnp.pad(term, ((lag_step, 0), (0, 0), (0, 0)))
    long_cols = jnp.einsum(
        "bck,ak->abc", mixed_spec.astype(jnp.bfloat16), back_table,
        preferred_element_type=jnp.float32,
    ).astype(jnp.bfloat16)

    grad_spec = jnp.einsum(
        "abc,ak->bck", grad_long_cols, back_table, preferred_element_type=jnp.float32
    ).astype(jnp.bfloat16)
    spectral_grad = jnp.zeros(grad_spec.shape, jnp.float32)
    filter_parts = []
    for lag_step in range(seq_count):
        ahead = grad_spec[lag_step:]
        term = spectral_adjoint(filters[lag_step][None], ahead)
        spectral_grad = spectral_grad + jnp.pad(term, ((0, lag_step), (0, 0), (0, 0)))
        filter_parts.append(
            jnp.sum(spectral_adjoint(own_spec[: seq_count - lag_step], ahead), axis=0)
        )
    filter_grad = jnp.stack(filter_parts, axis=0)
    gated_grad_cols = jnp.einsum(
        "bck,kt->tbc", spectral_grad.astype(jnp.bfloat16), half_table,
        preferred_element_type=jnp.float32,
    ).astype(jnp.bfloat16)

    tap_spec = jnp.einsum("dck,kn->dcn", filter_grad, forward, precision=lax.Precision.HIGHEST)
    tap_cols = tap_spec[:, :, row_count:] + jnp.concatenate(
        [tap_spec[1:, :, :row_count], jnp.zeros((1, group, row_count), jnp.float32)], axis=0
    )
    tap_cols = tap_cols.transpose(2, 0, 1).astype(jnp.bfloat16)

    def with_next_rows(cols):
        following = jnp.concatenate(
            [cols[:2, 1:], jnp.zeros((2, 1, group), cols.dtype)], axis=1
        )
        return jnp.concatenate([cols, following], axis=0)

    returned = swap_layout(
        jnp.concatenate(
            [
                with_next_rows(long_cols),
                with_next_rows(gated_grad_cols),
                jnp.concatenate([tap_cols, jnp.zeros((2, seq_count, group), jnp.bfloat16)], axis=0),
            ],
            axis=2,
        )
    )
    wide_rows = row_count + 2
    long_out = returned[..., :group].reshape(wide_rows, local_width).astype(jnp.float32)
    gated_wide = returned[..., group : 2 * group].reshape(wide_rows, local_width).astype(jnp.float32)
    tap_grads = returned[:row_count, :, 2 * group :].astype(jnp.float32).reshape(row_count, local_width)

    operator_out = (query_conv[:row_count] * long_out[:row_count]).astype(jnp.bfloat16)
    grad_query = cot_wide * long_out
    grad_streams = jnp.stack(
        [grad_query, gated_wide * value_conv, gated_wide * key_conv], axis=0
    ).astype(jnp.bfloat16).astype(jnp.float32)
    stream_grads = (
        conv_weight[:, 0] * grad_streams[:, :row_count]
        + conv_weight[:, 1] * grad_streams[:, 1 : row_count + 1]
        + conv_weight[:, 2] * grad_streams[:, 2:]
    ).astype(jnp.bfloat16).transpose(1, 0, 2)
    return (operator_out, stream_grads, tap_grads)


def solution(mesh):
    return jax.shard_map(
        on_device,
        mesh=mesh,
        in_specs=(
            P("seq", "chan"),
            P(None, None, "chan"),
            P(None, None, "chan"),
            P(None, "chan"),
            P("seq", "chan"),
        ),
        out_specs=(P("seq", "chan"), P("seq", None, "chan"), P("seq", "chan")),
        check_vma=False,
    )
```

```python
import math

import jax
import jax.numpy as jnp
from jax import lax
from jax.sharding import PartitionSpec as P


def passed_along(block, axis, distance):
    devices = range(lax.axis_size(axis))
    route = [(i - distance, i) for i in devices if i - distance in devices]
    return lax.ppermute(block, axis, route)


def dft_tables(row_count):
    length = 2 * row_count
    sample = jnp.arange(length, dtype=jnp.int32)
    frequency = jnp.arange(row_count, dtype=jnp.int32)
    angles = (frequency[:, None] * sample[None, :] % length).astype(jnp.float32) * (
        2.0 * math.pi / length
    )
    parity = 1.0 - 2.0 * (sample % 2).astype(jnp.float32)
    lower_rows = jnp.where(frequency[:, None] == 0, parity[None, :], -jnp.sin(angles))
    forward = jnp.concatenate([jnp.cos(angles), lower_rows], axis=0)
    out_index = row_count + frequency
    back_angles = (out_index[:, None] * frequency[None, :] % length).astype(jnp.float32) * (
        2.0 * math.pi / length
    )
    factor = jnp.where(frequency == 0, 1.0, 2.0) / length
    out_parity = 1.0 - 2.0 * (out_index % 2).astype(jnp.float32)
    real_part = jnp.cos(back_angles) * factor[None, :]
    imag_part = jnp.where(
        frequency[None, :] == 0, out_parity[:, None] / length, -2.0 * jnp.sin(back_angles) / length
    )
    inverse = jnp.concatenate([real_part, imag_part], axis=1)
    return (forward, inverse)


def spectral_product(left_spec, right_spec):
    half_len = left_spec.shape[-1] // 2
    left_spec = left_spec.astype(jnp.float32)
    right_spec = right_spec.astype(jnp.float32)
    left_re, left_im = (left_spec[..., :half_len], left_spec[..., half_len:])
    right_re, right_im = (right_spec[..., :half_len], right_spec[..., half_len:])
    first_row = lax.broadcasted_iota(jnp.int32, (1,) * (left_spec.ndim - 1) + (half_len,), left_spec.ndim - 1) == 0
    cross_term = left_im * right_im
    real_out = left_re * right_re - jnp.where(first_row, 0.0, cross_term)
    imag_out = jnp.where(first_row, cross_term, left_re * right_im + left_im * right_re)
    return jnp.concatenate([real_out, imag_out], axis=-1)


def spectral_adjoint(left_spec, grad_spec):
    half_len = left_spec.shape[-1] // 2
    left_spec = left_spec.astype(jnp.float32)
    grad_spec = grad_spec.astype(jnp.float32)
    left_re, left_im = (left_spec[..., :half_len], left_spec[..., half_len:])
    grad_re, grad_im = (grad_spec[..., :half_len], grad_spec[..., half_len:])
    first_row = lax.broadcasted_iota(jnp.int32, (1,) * (left_spec.ndim - 1) + (half_len,), left_spec.ndim - 1) == 0
    cross_term = left_im * grad_im
    real_out = left_re * grad_re + jnp.where(first_row, 0.0, cross_term)
    imag_out = jnp.where(first_row, cross_term, left_re * grad_im - left_im * grad_re)
    return jnp.concatenate([real_out, imag_out], axis=-1)


def neighbour_rows(edge_rows, offset):
    return passed_along(edge_rows, "seq", offset)


def swap_layout(values):
    return lax.all_to_all(values, "seq", 1, 1, tiled=True)


def on_device(tokens, in_weight, short_weight, filter_taps, cotangent):
    row_count, local_width = tokens.shape
    seq_count = lax.axis_size("seq")
    chan_count = lax.axis_size("chan")
    group = local_width // seq_count
    own_block = lax.axis_index("seq")
    forward, inverse = dft_tables(row_count)
    full_table = forward.astype(jnp.bfloat16)
    half_table = full_table[:, :row_count]
    back_table = inverse.astype(jnp.bfloat16)

    half_count = chan_count // 2
    core = lax.axis_index("chan") % 2
    groups = [[2 * j + k for j in range(half_count)] for k in range(2)]
    copies = jnp.broadcast_to(tokens[None], (half_count,) + tokens.shape)
    same_core = lax.all_to_all(copies, "chan", 0, 0, tiled=True, axis_index_groups=groups)
    other_core = lax.ppermute(same_core, "chan", [(i, i ^ 1) for i in range(chan_count)])
    weight_pairs = in_weight.reshape(half_count, 2, local_width, 3, local_width)
    own_weights = lax.dynamic_index_in_dim(weight_pairs, core, axis=1, keepdims=False)
    other_weights = lax.dynamic_index_in_dim(weight_pairs, 1 - core, axis=1, keepdims=False)
    streams = (
        jnp.einsum("stf,sfqc->qtc", same_core, own_weights, preferred_element_type=jnp.float32)
        + jnp.einsum(
            "stf,sfqc->qtc", other_core, other_weights, preferred_element_type=jnp.float32
        )
    ).astype(jnp.bfloat16)
    tail_rows = (
        jnp.einsum(
            "stf,sfqc->qtc", same_core[:, row_count - 2 :], own_weights,
            preferred_element_type=jnp.float32,
        )
        + jnp.einsum(
            "stf,sfqc->qtc", other_core[:, row_count - 2 :], other_weights,
            preferred_element_type=jnp.float32,
        )
    ).astype(jnp.bfloat16)
    before = neighbour_rows(tail_rows, 1)
    extended = jnp.concatenate([before, streams], axis=1).astype(jnp.float32)
    conv_weight = short_weight[:, :, None, :]
    conv_out = (
        conv_weight[:, 0] * extended[:, 2:]
        + conv_weight[:, 1] * extended[:, 1:-1]
        + conv_weight[:, 2] * extended[:, :-2]
    )
    query_conv, key_conv, value_conv = (conv_out[0], conv_out[1], conv_out[2])
    gated = (key_conv * value_conv).astype(jnp.bfloat16)
    grad_long = (cotangent.astype(jnp.float32) * query_conv).astype(jnp.bfloat16)

    both_cols = swap_layout(
        jnp.concatenate(
            [gated.reshape(row_count, seq_count, group), grad_long.reshape(row_count, seq_count, group)],
            axis=2,
        )
    )
    gated_cols, grad_long_cols = (both_cols[..., :group], both_cols[..., group:])

    after_rows, _ = lax.optimization_barrier(
        (jnp.concatenate([streams[:, :2], cotangent[None, :2]], axis=0), both_cols)
    )
    after = neighbour_rows(after_rows, -1)
    next_streams, next_cot = (after[:3], after[3])
    edge = jnp.concatenate([streams[:, row_count - 2 :], next_streams], axis=1).astype(jnp.float32)
    edge_out = (
        conv_weight[:, 0] * edge[:, 2:]
        + conv_weight[:, 1] * edge[:, 1:-1]
        + conv_weight[:, 2] * edge[:, :-2]
    )
    query_conv = jnp.concatenate([query_conv, edge_out[0]], axis=0)
    key_conv = jnp.concatenate([key_conv, edge_out[1]], axis=0)
    value_conv = jnp.concatenate([value_conv, edge_out[2]], axis=0)
    cot_wide = jnp.concatenate([cotangent, next_cot], axis=0).astype(jnp.float32)
    own_spec = jnp.einsum(
        "tbc,kt->bck", gated_cols, half_table, preferred_element_type=jnp.float32
    ).astype(jnp.bfloat16)
    own_taps = lax.dynamic_slice_in_dim(filter_taps, own_block * group, group, axis=1)
    tap_blocks = own_taps.reshape(seq_count, row_count, group)
    earlier = jnp.concatenate(
        [jnp.zeros((1, row_count, group), jnp.bfloat16), tap_blocks[:-1]], axis=0
    )
    segments = jnp.concatenate([earlier, tap_blocks], axis=1)
    filters = jnp.einsum(
        "fn,bnc->bcf", full_table, segments, preferred_element_type=jnp.float32
    ).astype(jnp.bfloat16)

    mixed_spec = jnp.zeros(own_spec.shape, jnp.float32)
    for lag_step in range(seq_count):
        term = spectral_product(filters[lag_step][None], own_spec[: seq_count - lag_step])
        mixed_spec = mixed_spec + jnp.pad(term, ((lag_step, 0), (0, 0), (0, 0)))
    long_cols = jnp.einsum(
        "bck,ak->abc", mixed_spec.astype(jnp.bfloat16), back_table,
        preferred_element_type=jnp.float32,
    ).astype(jnp.bfloat16)

    grad_spec = jnp.einsum(
        "abc,ak->bck", grad_long_cols, back_table, preferred_element_type=jnp.float32
    ).astype(jnp.bfloat16)
    spectral_grad = jnp.zeros(grad_spec.shape, jnp.float32)
    filter_parts = []
    for lag_step in range(seq_count):
        ahead = grad_spec[lag_step:]
        term = spectral_adjoint(filters[lag_step][None], ahead)
        spectral_grad = spectral_grad + jnp.pad(term, ((0, lag_step), (0, 0), (0, 0)))
        filter_parts.append(
            jnp.sum(spectral_adjoint(own_spec[: seq_count - lag_step], ahead), axis=0)
        )
    filter_grad = jnp.stack(filter_parts, axis=0)
    gated_grad_cols = jnp.einsum(
        "bck,kt->tbc", spectral_grad.astype(jnp.bfloat16), half_table,
        preferred_element_type=jnp.float32,
    ).astype(jnp.bfloat16)

    tap_spec = jnp.einsum("dck,kn->dcn", filter_grad, forward, precision=lax.Precision.HIGHEST)
    tap_cols = tap_spec[:, :, row_count:] + jnp.concatenate(
        [tap_spec[1:, :, :row_count], jnp.zeros((1, group, row_count), jnp.float32)], axis=0
    )
    tap_cols = tap_cols.transpose(2, 0, 1).astype(jnp.bfloat16)

    def with_next_rows(cols):
        following = jnp.concatenate(
            [cols[:2, 1:], jnp.zeros((2, 1, group), cols.dtype)], axis=1
        )
        return jnp.concatenate([cols, following], axis=0)

    returned = swap_layout(
        jnp.concatenate(
            [
                with_next_rows(long_cols),
                with_next_rows(gated_grad_cols),
                jnp.concatenate([tap_cols, jnp.zeros((2, seq_count, group), jnp.bfloat16)], axis=0),
            ],
            axis=2,
        )
    )
    wide_rows = row_count + 2
    long_out = returned[..., :group].reshape(wide_rows, local_width).astype(jnp.float32)
    gated_wide = returned[..., group : 2 * group].reshape(wide_rows, local_width).astype(jnp.float32)
    tap_grads = returned[:row_count, :, 2 * group :].astype(jnp.float32).reshape(row_count, local_width)

    operator_out = (query_conv[:row_count] * long_out[:row_count]).astype(jnp.bfloat16)
    grad_query = cot_wide * long_out
    grad_streams = jnp.stack(
        [grad_query, gated_wide * value_conv, gated_wide * key_conv], axis=0
    ).astype(jnp.bfloat16).astype(jnp.float32)
    stream_grads = (
        conv_weight[:, 0] * grad_streams[:, :row_count]
        + conv_weight[:, 1] * grad_streams[:, 1 : row_count + 1]
        + conv_weight[:, 2] * grad_streams[:, 2:]
    ).astype(jnp.bfloat16).transpose(1, 0, 2)
    return (operator_out, stream_grads, tap_grads)


def solution(mesh):
    return jax.shard_map(
        on_device,
        mesh=mesh,
        in_specs=(
            P("seq", "chan"),
            P(None, None, "chan"),
            P(None, None, "chan"),
            P(None, "chan"),
            P("seq", "chan"),
        ),
        out_specs=(P("seq", "chan"), P("seq", None, "chan"), P("seq", "chan")),
        check_vma=False,
    )
```

```python
import math

import jax
import jax.numpy as jnp
from jax import lax
from jax.sharding import PartitionSpec as P


def passed_along(block, axis, distance):
    devices = range(lax.axis_size(axis))
    route = [(i - distance, i) for i in devices if i - distance in devices]
    return lax.ppermute(block, axis, route)


def dft_tables(row_count):
    length = 2 * row_count
    sample = jnp.arange(length, dtype=jnp.int32)
    frequency = jnp.arange(row_count, dtype=jnp.int32)
    angles = (frequency[:, None] * sample[None, :] % length).astype(jnp.float32) * (
        2.0 * math.pi / length
    )
    parity = 1.0 - 2.0 * (sample % 2).astype(jnp.float32)
    lower_rows = jnp.where(frequency[:, None] == 0, parity[None, :], -jnp.sin(angles))
    forward = jnp.concatenate([jnp.cos(angles), lower_rows], axis=0)
    out_index = row_count + frequency
    back_angles = (out_index[:, None] * frequency[None, :] % length).astype(jnp.float32) * (
        2.0 * math.pi / length
    )
    factor = jnp.where(frequency == 0, 1.0, 2.0) / length
    out_parity = 1.0 - 2.0 * (out_index % 2).astype(jnp.float32)
    real_part = jnp.cos(back_angles) * factor[None, :]
    imag_part = jnp.where(
        frequency[None, :] == 0, out_parity[:, None] / length, -2.0 * jnp.sin(back_angles) / length
    )
    inverse = jnp.concatenate([real_part, imag_part], axis=1)
    return (forward, inverse)


def spectral_product(left_spec, right_spec):
    half_len = left_spec.shape[-1] // 2
    left_spec = left_spec.astype(jnp.float32)
    right_spec = right_spec.astype(jnp.float32)
    left_re, left_im = (left_spec[..., :half_len], left_spec[..., half_len:])
    right_re, right_im = (right_spec[..., :half_len], right_spec[..., half_len:])
    first_row = lax.broadcasted_iota(jnp.int32, (1,) * (left_spec.ndim - 1) + (half_len,), left_spec.ndim - 1) == 0
    cross_term = left_im * right_im
    real_out = left_re * right_re - jnp.where(first_row, 0.0, cross_term)
    imag_out = jnp.where(first_row, cross_term, left_re * right_im + left_im * right_re)
    return jnp.concatenate([real_out, imag_out], axis=-1)


def spectral_adjoint(left_spec, grad_spec):
    half_len = left_spec.shape[-1] // 2
    left_spec = left_spec.astype(jnp.float32)
    grad_spec = grad_spec.astype(jnp.float32)
    left_re, left_im = (left_spec[..., :half_len], left_spec[..., half_len:])
    grad_re, grad_im = (grad_spec[..., :half_len], grad_spec[..., half_len:])
    first_row = lax.broadcasted_iota(jnp.int32, (1,) * (left_spec.ndim - 1) + (half_len,), left_spec.ndim - 1) == 0
    cross_term = left_im * grad_im
    real_out = left_re * grad_re + jnp.where(first_row, 0.0, cross_term)
    imag_out = jnp.where(first_row, cross_term, left_re * grad_im - left_im * grad_re)
    return jnp.concatenate([real_out, imag_out], axis=-1)


def neighbour_rows(edge_rows, offset):
    return passed_along(edge_rows, "seq", offset)


def swap_layout(values):
    return lax.all_to_all(values, "seq", 1, 1, tiled=True)


def on_device(tokens, in_weight, short_weight, filter_taps, cotangent):
    row_count, local_width = tokens.shape
    seq_count = lax.axis_size("seq")
    chan_count = lax.axis_size("chan")
    group = local_width // seq_count
    own_block = lax.axis_index("seq")
    forward, inverse = dft_tables(row_count)
    full_table = forward.astype(jnp.bfloat16)
    half_table = full_table[:, :row_count]
    back_table = inverse.astype(jnp.bfloat16)

    half_count = chan_count // 2
    core = lax.axis_index("chan") % 2
    groups = [[2 * j + k for j in range(half_count)] for k in range(2)]
    copies = jnp.broadcast_to(tokens[None], (half_count,) + tokens.shape)
    same_core = lax.all_to_all(copies, "chan", 0, 0, tiled=True, axis_index_groups=groups)
    other_core = lax.ppermute(same_core, "chan", [(i, i ^ 1) for i in range(chan_count)])
    weight_pairs = in_weight.reshape(half_count, 2, local_width, 3, local_width)
    own_weights = lax.dynamic_index_in_dim(weight_pairs, core, axis=1, keepdims=False)
    other_weights = lax.dynamic_index_in_dim(weight_pairs, 1 - core, axis=1, keepdims=False)
    streams = (
        jnp.einsum("stf,sfqc->qtc", same_core, own_weights, preferred_element_type=jnp.float32)
        + jnp.einsum(
            "stf,sfqc->qtc", other_core, other_weights, preferred_element_type=jnp.float32
        )
    ).astype(jnp.bfloat16)
    tail_rows = (
        jnp.einsum(
            "stf,sfqc->qtc", same_core[:, row_count - 2 :], own_weights,
            preferred_element_type=jnp.float32,
        )
        + jnp.einsum(
            "stf,sfqc->qtc", other_core[:, row_count - 2 :], other_weights,
            preferred_element_type=jnp.float32,
        )
    ).astype(jnp.bfloat16)
    before = neighbour_rows(tail_rows, 1)
    extended = jnp.concatenate([before, streams], axis=1).astype(jnp.float32)
    conv_weight = short_weight[:, :, None, :]
    conv_out = (
        conv_weight[:, 0] * extended[:, 2:]
        + conv_weight[:, 1] * extended[:, 1:-1]
        + conv_weight[:, 2] * extended[:, :-2]
    )
    query_conv, key_conv, value_conv = (conv_out[0], conv_out[1], conv_out[2])
    gated = (key_conv * value_conv).astype(jnp.bfloat16)
    grad_long = (cotangent.astype(jnp.float32) * query_conv).astype(jnp.bfloat16)

    both_cols = swap_layout(
        jnp.concatenate([gated, grad_long], axis=0).reshape(2 * row_count, seq_count, group)
    )
    gated_cols, grad_long_cols = (both_cols[:row_count], both_cols[row_count:])

    after_rows, _ = lax.optimization_barrier(
        (jnp.concatenate([streams[:, :2], cotangent[None, :2]], axis=0), both_cols)
    )
    after = neighbour_rows(after_rows, -1)
    next_streams, next_cot = (after[:3], after[3])
    edge = jnp.concatenate([streams[:, row_count - 2 :], next_streams], axis=1).astype(jnp.float32)
    edge_out = (
        conv_weight[:, 0] * edge[:, 2:]
        + conv_weight[:, 1] * edge[:, 1:-1]
        + conv_weight[:, 2] * edge[:, :-2]
    )
    query_conv = jnp.concatenate([query_conv, edge_out[0]], axis=0)
    key_conv = jnp.concatenate([key_conv, edge_out[1]], axis=0)
    value_conv = jnp.concatenate([value_conv, edge_out[2]], axis=0)
    cot_wide = jnp.concatenate([cotangent, next_cot], axis=0).astype(jnp.float32)
    own_spec = jnp.einsum(
        "tbc,kt->bck", gated_cols, half_table, preferred_element_type=jnp.float32
    ).astype(jnp.bfloat16)
    own_taps = lax.dynamic_slice_in_dim(filter_taps, own_block * group, group, axis=1)
    tap_blocks = own_taps.reshape(seq_count, row_count, group)
    earlier = jnp.concatenate(
        [jnp.zeros((1, row_count, group), jnp.bfloat16), tap_blocks[:-1]], axis=0
    )
    segments = jnp.concatenate([earlier, tap_blocks], axis=1)
    filters = jnp.einsum(
        "fn,bnc->bcf", full_table, segments, preferred_element_type=jnp.float32
    ).astype(jnp.bfloat16)

    mixed_spec = jnp.zeros(own_spec.shape, jnp.float32)
    for lag_step in range(seq_count):
        term = spectral_product(filters[lag_step][None], own_spec[: seq_count - lag_step])
        mixed_spec = mixed_spec + jnp.pad(term, ((lag_step, 0), (0, 0), (0, 0)))
    long_cols = jnp.einsum(
        "bck,ak->abc", mixed_spec.astype(jnp.bfloat16), back_table,
        preferred_element_type=jnp.float32,
    ).astype(jnp.bfloat16)

    grad_spec = jnp.einsum(
        "abc,ak->bck", grad_long_cols, back_table, preferred_element_type=jnp.float32
    ).astype(jnp.bfloat16)
    spectral_grad = jnp.zeros(grad_spec.shape, jnp.float32)
    filter_parts = []
    for lag_step in range(seq_count):
        ahead = grad_spec[lag_step:]
        term = spectral_adjoint(filters[lag_step][None], ahead)
        spectral_grad = spectral_grad + jnp.pad(term, ((0, lag_step), (0, 0), (0, 0)))
        filter_parts.append(
            jnp.sum(spectral_adjoint(own_spec[: seq_count - lag_step], ahead), axis=0)
        )
    filter_grad = jnp.stack(filter_parts, axis=0)
    gated_grad_cols = jnp.einsum(
        "bck,kt->tbc", spectral_grad.astype(jnp.bfloat16), half_table,
        preferred_element_type=jnp.float32,
    ).astype(jnp.bfloat16)

    tap_spec = jnp.einsum("dck,kn->dcn", filter_grad, forward, precision=lax.Precision.HIGHEST)
    tap_cols = tap_spec[:, :, row_count:] + jnp.concatenate(
        [tap_spec[1:, :, :row_count], jnp.zeros((1, group, row_count), jnp.float32)], axis=0
    )
    tap_cols = tap_cols.transpose(2, 0, 1).astype(jnp.bfloat16)

    def with_next_rows(cols):
        following = jnp.concatenate(
            [cols[:2, 1:], jnp.zeros((2, 1, group), cols.dtype)], axis=1
        )
        return jnp.concatenate([cols, following], axis=0)

    returned = swap_layout(
        jnp.concatenate(
            [
                with_next_rows(long_cols),
                with_next_rows(gated_grad_cols),
                jnp.concatenate([tap_cols, jnp.zeros((2, seq_count, group), jnp.bfloat16)], axis=0),
            ],
            axis=2,
        )
    )
    wide_rows = row_count + 2
    long_out = returned[..., :group].reshape(wide_rows, local_width).astype(jnp.float32)
    gated_wide = returned[..., group : 2 * group].reshape(wide_rows, local_width).astype(jnp.float32)
    tap_grads = returned[:row_count, :, 2 * group :].astype(jnp.float32).reshape(row_count, local_width)

    operator_out = (query_conv[:row_count] * long_out[:row_count]).astype(jnp.bfloat16)
    grad_query = cot_wide * long_out
    grad_streams = jnp.stack(
        [grad_query, gated_wide * value_conv, gated_wide * key_conv], axis=0
    ).astype(jnp.bfloat16).astype(jnp.float32)
    stream_grads = (
        conv_weight[:, 0] * grad_streams[:, :row_count]
        + conv_weight[:, 1] * grad_streams[:, 1 : row_count + 1]
        + conv_weight[:, 2] * grad_streams[:, 2:]
    ).astype(jnp.bfloat16).transpose(1, 0, 2)
    return (operator_out, stream_grads, tap_grads)


def solution(mesh):
    return jax.shard_map(
        on_device,
        mesh=mesh,
        in_specs=(
            P("seq", "chan"),
            P(None, None, "chan"),
            P(None, None, "chan"),
            P(None, "chan"),
            P("seq", "chan"),
        ),
        out_specs=(P("seq", "chan"), P("seq", None, "chan"), P("seq", "chan")),
        check_vma=False,
    )
```

```python
import math

import jax
import jax.numpy as jnp
from jax import lax
from jax.sharding import PartitionSpec as P


def passed_along(block, axis, distance):
    devices = range(lax.axis_size(axis))
    route = [(i - distance, i) for i in devices if i - distance in devices]
    return lax.ppermute(block, axis, route)


def dft_tables(row_count):
    length = 2 * row_count
    sample = jnp.arange(length, dtype=jnp.int32)
    frequency = jnp.arange(row_count, dtype=jnp.int32)
    angles = (frequency[:, None] * sample[None, :] % length).astype(jnp.float32) * (
        2.0 * math.pi / length
    )
    parity = 1.0 - 2.0 * (sample % 2).astype(jnp.float32)
    lower_rows = jnp.where(frequency[:, None] == 0, parity[None, :], -jnp.sin(angles))
    forward = jnp.concatenate([jnp.cos(angles), lower_rows], axis=0)
    out_index = row_count + frequency
    back_angles = (out_index[:, None] * frequency[None, :] % length).astype(jnp.float32) * (
        2.0 * math.pi / length
    )
    factor = jnp.where(frequency == 0, 1.0, 2.0) / length
    out_parity = 1.0 - 2.0 * (out_index % 2).astype(jnp.float32)
    real_part = jnp.cos(back_angles) * factor[None, :]
    imag_part = jnp.where(
        frequency[None, :] == 0, out_parity[:, None] / length, -2.0 * jnp.sin(back_angles) / length
    )
    inverse = jnp.concatenate([real_part, imag_part], axis=1)
    return (forward, inverse)


def spectral_product(left_spec, right_spec):
    half_len = left_spec.shape[-1] // 2
    left_spec = left_spec.astype(jnp.float32)
    right_spec = right_spec.astype(jnp.float32)
    left_re, left_im = (left_spec[..., :half_len], left_spec[..., half_len:])
    right_re, right_im = (right_spec[..., :half_len], right_spec[..., half_len:])
    first_row = lax.broadcasted_iota(jnp.int32, (1,) * (left_spec.ndim - 1) + (half_len,), left_spec.ndim - 1) == 0
    cross_term = left_im * right_im
    real_out = left_re * right_re - jnp.where(first_row, 0.0, cross_term)
    imag_out = jnp.where(first_row, cross_term, left_re * right_im + left_im * right_re)
    return jnp.concatenate([real_out, imag_out], axis=-1)


def spectral_adjoint(left_spec, grad_spec):
    half_len = left_spec.shape[-1] // 2
    left_spec = left_spec.astype(jnp.float32)
    grad_spec = grad_spec.astype(jnp.float32)
    left_re, left_im = (left_spec[..., :half_len], left_spec[..., half_len:])
    grad_re, grad_im = (grad_spec[..., :half_len], grad_spec[..., half_len:])
    first_row = lax.broadcasted_iota(jnp.int32, (1,) * (left_spec.ndim - 1) + (half_len,), left_spec.ndim - 1) == 0
    cross_term = left_im * grad_im
    real_out = left_re * grad_re + jnp.where(first_row, 0.0, cross_term)
    imag_out = jnp.where(first_row, cross_term, left_re * grad_im - left_im * grad_re)
    return jnp.concatenate([real_out, imag_out], axis=-1)


def neighbour_rows(edge_rows, offset):
    return passed_along(edge_rows, "seq", offset)


def swap_layout(values):
    return lax.all_to_all(values, "seq", 1, 1, tiled=True)


def on_device(tokens, in_weight, short_weight, filter_taps, cotangent):
    row_count, local_width = tokens.shape
    seq_count = lax.axis_size("seq")
    chan_count = lax.axis_size("chan")
    group = local_width // seq_count
    own_block = lax.axis_index("seq")
    forward, inverse = dft_tables(row_count)
    full_table = forward.astype(jnp.bfloat16)
    half_table = full_table[:, :row_count]
    back_table = inverse.astype(jnp.bfloat16)

    half_count = chan_count // 2
    core = lax.axis_index("chan") % 2
    groups = [[2 * j + k for j in range(half_count)] for k in range(2)]
    copies = jnp.broadcast_to(tokens[None], (half_count,) + tokens.shape)
    same_core = lax.all_to_all(copies, "chan", 0, 0, tiled=True, axis_index_groups=groups)
    other_core = lax.ppermute(same_core, "chan", [(i, i ^ 1) for i in range(chan_count)])
    weight_pairs = in_weight.reshape(half_count, 2, local_width, 3, local_width)
    own_weights = lax.dynamic_index_in_dim(weight_pairs, core, axis=1, keepdims=False)
    other_weights = lax.dynamic_index_in_dim(weight_pairs, 1 - core, axis=1, keepdims=False)
    streams = (
        jnp.einsum("stf,sfqc->qtc", same_core, own_weights, preferred_element_type=jnp.float32)
        + jnp.einsum(
            "stf,sfqc->qtc", other_core, other_weights, preferred_element_type=jnp.float32
        )
    ).astype(jnp.bfloat16)
    tail_rows = (
        jnp.einsum(
            "stf,sfqc->qtc", same_core[:, row_count - 2 :], own_weights,
            preferred_element_type=jnp.float32,
        )
        + jnp.einsum(
            "stf,sfqc->qtc", other_core[:, row_count - 2 :], other_weights,
            preferred_element_type=jnp.float32,
        )
    ).astype(jnp.bfloat16)
    before = neighbour_rows(tail_rows, 1)
    extended = jnp.concatenate([before, streams], axis=1).astype(jnp.float32)
    conv_weight = short_weight[:, :, None, :]
    conv_out = (
        conv_weight[:, 0] * extended[:, 2:]
        + conv_weight[:, 1] * extended[:, 1:-1]
        + conv_weight[:, 2] * extended[:, :-2]
    )
    query_conv, key_conv, value_conv = (conv_out[0], conv_out[1], conv_out[2])
    gated = (key_conv * value_conv).astype(jnp.bfloat16)
    grad_long = (cotangent.astype(jnp.float32) * query_conv).astype(jnp.bfloat16)

    both_cols = swap_layout(
        jnp.concatenate([gated, grad_long], axis=0).reshape(2 * row_count, seq_count, group)
    )
    gated_cols, grad_long_cols = (both_cols[:row_count], both_cols[row_count:])

    after_rows, _ = lax.optimization_barrier(
        (jnp.concatenate([streams[:, :2], cotangent[None, :2]], axis=0), both_cols)
    )
    after = neighbour_rows(after_rows, -1)
    next_streams, next_cot = (after[:3], after[3])
    edge = jnp.concatenate([streams[:, row_count - 2 :], next_streams], axis=1).astype(jnp.float32)
    edge_out = (
        conv_weight[:, 0] * edge[:, 2:]
        + conv_weight[:, 1] * edge[:, 1:-1]
        + conv_weight[:, 2] * edge[:, :-2]
    )
    query_conv = jnp.concatenate([query_conv, edge_out[0]], axis=0)
    key_conv = jnp.concatenate([key_conv, edge_out[1]], axis=0)
    value_conv = jnp.concatenate([value_conv, edge_out[2]], axis=0)
    cot_wide = jnp.concatenate([cotangent, next_cot], axis=0).astype(jnp.float32)
    own_spec = jnp.einsum(
        "tbc,kt->bck", gated_cols, half_table, preferred_element_type=jnp.float32
    ).astype(jnp.bfloat16)
    own_taps = lax.dynamic_slice_in_dim(filter_taps, own_block * group, group, axis=1)
    tap_blocks = own_taps.reshape(seq_count, row_count, group)
    earlier = jnp.concatenate(
        [jnp.zeros((1, row_count, group), jnp.bfloat16), tap_blocks[:-1]], axis=0
    )
    segments = jnp.concatenate([earlier, tap_blocks], axis=1)
    filters = jnp.einsum(
        "fn,bnc->bcf", full_table, segments, preferred_element_type=jnp.float32
    ).astype(jnp.bfloat16)

    mixed_spec = jnp.zeros(own_spec.shape, jnp.float32)
    for lag_step in range(seq_count):
        term = spectral_product(filters[lag_step][None], own_spec[: seq_count - lag_step])
        mixed_spec = mixed_spec + jnp.pad(term, ((lag_step, 0), (0, 0), (0, 0)))
    long_cols = jnp.einsum(
        "bck,ak->abc", mixed_spec.astype(jnp.bfloat16), back_table,
        preferred_element_type=jnp.float32,
    ).astype(jnp.bfloat16)

    grad_spec = jnp.einsum(
        "abc,ak->bck", grad_long_cols, back_table, preferred_element_type=jnp.float32
    ).astype(jnp.bfloat16)
    spectral_grad = jnp.zeros(grad_spec.shape, jnp.float32)
    filter_parts = []
    for lag_step in range(seq_count):
        ahead = grad_spec[lag_step:]
        term = spectral_adjoint(filters[lag_step][None], ahead)
        spectral_grad = spectral_grad + jnp.pad(term, ((0, lag_step), (0, 0), (0, 0)))
        filter_parts.append(
            jnp.sum(spectral_adjoint(own_spec[: seq_count - lag_step], ahead), axis=0)
        )
    filter_grad = jnp.stack(filter_parts, axis=0)
    gated_grad_cols = jnp.einsum(
        "bck,kt->tbc", spectral_grad.astype(jnp.bfloat16), half_table,
        preferred_element_type=jnp.float32,
    ).astype(jnp.bfloat16)

    tap_spec = jnp.einsum("dck,kn->dcn", filter_grad, forward, precision=lax.Precision.HIGHEST)
    tap_cols = tap_spec[:, :, row_count:] + jnp.concatenate(
        [tap_spec[1:, :, :row_count], jnp.zeros((1, group, row_count), jnp.float32)], axis=0
    )
    tap_cols = tap_cols.transpose(2, 0, 1).astype(jnp.bfloat16)

    def with_next_rows(cols):
        following = jnp.concatenate(
            [cols[:2, 1:], jnp.zeros((2, 1, group), cols.dtype)], axis=1
        )
        return jnp.concatenate([cols, following], axis=0)

    wide_rows = row_count + 2
    returned = swap_layout(
        jnp.concatenate([with_next_rows(long_cols), with_next_rows(gated_grad_cols), tap_cols], axis=0)
    )
    long_out = returned[:wide_rows].reshape(wide_rows, local_width).astype(jnp.float32)
    gated_wide = returned[wide_rows : 2 * wide_rows].reshape(wide_rows, local_width).astype(jnp.float32)
    tap_grads = returned[2 * wide_rows :].astype(jnp.float32).reshape(row_count, local_width)

    operator_out = (query_conv[:row_count] * long_out[:row_count]).astype(jnp.bfloat16)
    grad_query = cot_wide * long_out
    grad_streams = jnp.stack(
        [grad_query, gated_wide * value_conv, gated_wide * key_conv], axis=0
    ).astype(jnp.bfloat16).astype(jnp.float32)
    stream_grads = (
        conv_weight[:, 0] * grad_streams[:, :row_count]
        + conv_weight[:, 1] * grad_streams[:, 1 : row_count + 1]
        + conv_weight[:, 2] * grad_streams[:, 2:]
    ).astype(jnp.bfloat16).transpose(1, 0, 2)
    return (operator_out, stream_grads, tap_grads)


def solution(mesh):
    return jax.shard_map(
        on_device,
        mesh=mesh,
        in_specs=(
            P("seq", "chan"),
            P(None, None, "chan"),
            P(None, None, "chan"),
            P(None, "chan"),
            P("seq", "chan"),
        ),
        out_specs=(P("seq", "chan"), P("seq", None, "chan"), P("seq", "chan")),
        check_vma=False,
    )
```
